32 devices in a mesh: gx: 4 (over y, x), gy: 8 (over z, core).
Axes of the slice: x: 2, y: 2, z: 4, core: 2. Of those that a mesh axis runs over, the one named last changes fastest.
Arguments:
- basis: float32 [4, 8, 3, 32, 192], P('gx', 'gy'), may hold values from -6 to 6
- coupling: bfloat16 [4, 8, 81, 192, 192], P('gx', 'gy'), as said below
- cpl_dst: int32 [4, 8, 81], P('gx', 'gy'), may hold values from 0 to 3, as said below
- cpl_src: int32 [4, 8, 81], P('gx', 'gy'), may hold values from 0 to 26, as said below
Outputs:
- subspace: float32 [4, 8, 3, 32, 192], P('gx', 'gy')
The draws below stay inside these ranges and needn't reach their ends.
Inputs may be any that keep to these rules, and one draw needn't show every extreme that they name: `cpl_dst`: on each column the live slots come first; a live slot holds its target block's height 0 to 2, every later slot holds 3. The columns at gx index 0 have all 81 slots live. `cpl_src`: A live slot holds (3 dx + dy) * 3 + z for a source block in the column at offsets dx - 1, dy - 1 (periodic) and height z, within one height of the target block, periodically; each source block and column offset appears at most once per target; empty slots hold 0. `coupling`: the assembled matrix is symmetric: for every live slot that couples block i to block j there is a live slot on j's column that couples j to i and holds the transposed block.
All inputs are finite; a program needn't handle non-finite values.
Results may differ from the reference program's by a relative error of at most 0.0085.
Values may be sent and summed in bfloat16 or wider, within the bound.
No kernel may reach another device: no remote copies, remote signals or barrier semaphores. Data moves between devices by JAX's collectives and lax.ppermute only.
A program may use at most 64 MiB of HBM per device.

```python
import math
import jax
import jax.numpy as jnp
from jax import lax

DOF = 192
VECTORS = 32
DEPTH = 3
DEGREE = 8
STEPS = 2
SLOTS = 81
N_GX = 4
N_GY = 8


def layout(key):
    bits = jax.random.randint(jax.random.fold_in(key, 11), (N_GX, N_GY, DEPTH, 27), 0, 2)
    codes = jnp.arange(27, dtype=jnp.int32)
    step_x = codes // 9 - 1
    step_y = codes // 3 % 3 - 1
    step_z = codes % 3 - 1
    pos_x = jnp.arange(N_GX, dtype=jnp.int32)[:, None, None, None]
    pos_y = jnp.arange(N_GY, dtype=jnp.int32)[None, :, None, None]
    pos_z = jnp.arange(DEPTH, dtype=jnp.int32)[None, None, :, None]
    near_edge = (pos_x == 0) | ((pos_x + step_x) % N_GX == 0)
    forward = (bits == 1) | near_edge
    other_x = jnp.broadcast_to((pos_x + step_x) % N_GX, (N_GX, N_GY, DEPTH, 27))
    other_y = jnp.broadcast_to((pos_y + step_y) % N_GY, (N_GX, N_GY, DEPTH, 27))
    other_z = jnp.broadcast_to((pos_z + step_z) % DEPTH, (N_GX, N_GY, DEPTH, 27))
    other_code = jnp.broadcast_to(26 - codes, (N_GX, N_GY, DEPTH, 27))
    mirror = forward[other_x, other_y, other_z, other_code]
    present = jnp.where(codes > 13, forward, jnp.where(codes == 13, True, mirror))
    flags = present.reshape(N_GX, N_GY, DEPTH * 27).astype(jnp.int32)
    places = jnp.cumsum(flags, axis=2) - 1
    places = jnp.where(flags == 1, places, SLOTS)
    item_z = jnp.repeat(jnp.arange(DEPTH, dtype=jnp.int32), 27)
    item_code = jnp.tile(codes, DEPTH)
    item_src = item_code // 3 * DEPTH + (item_z + item_code % 3 - 1) % DEPTH
    item_ids = jnp.arange(DEPTH * 27, dtype=jnp.int32)

    def fill_row(place_row, values, empty):
        return jnp.full((SLOTS,), empty, jnp.int32).at[place_row].set(values, mode='drop')

    def fill_all(values, empty):

        def inner(place_row):
            return fill_row(place_row, values, empty)
        return jax.vmap(jax.vmap(inner))(places)
    return (fill_all(item_z, DEPTH), fill_all(item_src, 0), fill_all(item_ids, 0))


def draw_cpl_dst(key, part):
    return layout(key)[0]


def draw_cpl_src(key, part):
    return layout(key)[1]


def draw_coupling(key, part):
    targets, sources, items = layout(key)
    weight_key = jax.random.fold_in(key, 23)
    diag_key = jax.random.fold_in(key, 29)
    scale = 1.0 / math.sqrt(DOF * 27 * 2)

    def raw_block(block_code):
        block_key = jax.random.fold_in(weight_key, block_code)
        return jax.random.normal(block_key, (DOF, DOF), jnp.float32)

    def one_block(column_x, column_y, item):
        height = item // 27
        code = item % 27
        step_x = code // 9 - 1
        step_y = code // 3 % 3 - 1
        step_z = code % 3 - 1
        block_id = (column_x * N_GY + column_y) * DEPTH + height
        other_id = ((column_x + step_x) % N_GX * N_GY + (column_y + step_y) % N_GY) * DEPTH + (height + step_z) % DEPTH
        first = raw_block(block_id * 27 + code)
        second = raw_block(other_id * 27 + 26 - code)
        diag_values = jax.random.uniform(jax.random.fold_in(diag_key, block_id), (DOF,), jnp.float32, 1.5, 6.0)
        diag_part = jnp.where(code == 13, 1.0, 0.0) * jnp.eye(DOF, dtype=jnp.float32) * diag_values[None, :]
        return (first + second.T) * scale + diag_part
    flat_items = items.reshape(N_GX * N_GY, SLOTS)

    def per_device(operands):
        index, item_row = operands
        column_x = index // N_GY
        column_y = index % N_GY

        def per_slot(item):
            return one_block(column_x, column_y, item)
        return jax.vmap(per_slot)(item_row).astype(jnp.bfloat16)
    blocks = lax.map(per_device, (jnp.arange(N_GX * N_GY, dtype=jnp.int32), flat_items))
    return blocks.reshape(N_GX, N_GY, SLOTS, DOF, DOF)


def shard_levels(rng, dims, cuts, least, largest):
    def one(dim, parts):
        heights = jax.random.uniform(jax.random.fold_in(jax.random.fold_in(rng, 6), dim), (parts,), jnp.float32, least / len(cuts), largest / len(cuts))
        return jnp.repeat(jnp.exp(heights), dims[dim] // parts).reshape((-1,) + (1,) * (len(dims) - dim - 1))

    level = one(*cuts[0])
    for cut in cuts[1:]:
        level = level * one(*cut)
    return level


def bell_draw(stream_key, shape, spread, bound, pieces=(), kind=jnp.bfloat16):
    array = spread * jax.random.normal(stream_key, shape, jnp.float32)
    if pieces:
        array = array * shard_levels(stream_key, shape, pieces, -0.22, 0.18)
    return jnp.clip(array, -bound, bound).astype(kind)


def setup_inputs(seed: int = 0) -> dict:
    splits = jax.random.split(jax.random.key(seed), 5)
    return {
        "basis": bell_draw(splits[0], (N_GX, N_GY, DEPTH, VECTORS, DOF), 1.0, 6.0, ((0, 4), (1, 8)), jnp.float32),
        "coupling": draw_coupling(jax.random.fold_in(splits[4], 71), 0),
        "cpl_dst": draw_cpl_dst(jax.random.fold_in(splits[4], 71), 0),
        "cpl_src": draw_cpl_src(jax.random.fold_in(splits[4], 71), 0),
    }


CENTER = 5.0
HALF = 3.0
LOWEST = 0.5

def apply_operator(current, coupling, cpl_dst, cpl_src):
    rounded = current.astype(jnp.bfloat16)
    columns = []
    for shift_x in (1, 0, -1):
        for shift_y in (1, 0, -1):
            columns.append(jnp.roll(rounded, (shift_x, shift_y), axis=(0, 1)))
    window = jnp.stack(columns, axis=2).reshape(N_GX * N_GY, 9 * DEPTH, VECTORS, DOF)
    matrices = coupling.reshape(N_GX * N_GY, SLOTS, DOF, DOF)
    targets = cpl_dst.reshape(N_GX * N_GY, SLOTS)
    sources = cpl_src.reshape(N_GX * N_GY, SLOTS)

    def one_device(operands):
        cells, matrix, target_row, source_row = operands
        picked = jnp.take(cells, source_row, axis=0).astype(jnp.float32)
        products = jnp.einsum('kvj,kij->kvi', picked, matrix.astype(jnp.float32), precision=lax.Precision.HIGHEST)
        select = (target_row[None, :] == jnp.arange(DEPTH, dtype=jnp.int32)[:, None]).astype(jnp.float32)
        return jnp.einsum('zk,kvi->zvi', select, products, precision=lax.Precision.HIGHEST)
    applied = lax.map(one_device, (window, matrices, targets, sources))
    return applied.reshape(N_GX, N_GY, DEPTH, VECTORS, DOF)

def reference(basis, coupling, cpl_dst, cpl_src):
    rows_total = N_GX * N_GY * DEPTH * DOF
    sigma_one = HALF / (LOWEST - CENTER)
    current_basis = basis
    for outer in range(STEPS):
        previous = current_basis
        current = sigma_one / HALF * (apply_operator(previous, coupling, cpl_dst, cpl_src) - CENTER * previous)
        sigma_now = sigma_one
        for inner in range(1, DEGREE):
            sigma_next = 1.0 / (2.0 / sigma_one - sigma_now)
            image = apply_operator(current, coupling, cpl_dst, cpl_src)
            following = 2.0 * sigma_next / HALF * (image - CENTER * current) - sigma_now * sigma_next * previous
            previous, current, sigma_now = (current, following, sigma_next)
        gram_matrix = jnp.einsum('abzvd,abzwd->vw', current, current, precision=lax.Precision.HIGHEST)
        factor = jnp.linalg.cholesky(gram_matrix)
        inverse = jax.scipy.linalg.solve_triangular(factor, jnp.eye(VECTORS, dtype=jnp.float32), lower=True)
        current_basis = jnp.einsum('vw,abzwd->abzvd', inverse, current, precision=lax.Precision.HIGHEST) * math.sqrt(rows_total)
    return current_basis
```

```python
import math

import jax
import jax.numpy as jnp
from jax import lax
from jax.experimental import pallas as pl
from jax.experimental.pallas import tpu as pltpu
from jax.sharding import PartitionSpec as P

DEGREE = 8
STEPS = 2


CENTER = 5.0
HALF = 3.0
LOWEST = 0.5

CHUNK = 9


def gather_window(rounded):
    nx = lax.axis_size("gx")
    ny = lax.axis_size("gy")
    cells = []
    for dx in range(3):
        for dy in range(3):
            if dx == 1 and dy == 1:
                cells.append(rounded)
                continue
            pairs = []
            for a in range(nx):
                for b in range(ny):
                    src = a * ny + b
                    dst = ((a - dx + 1) % nx) * ny + (b - dy + 1) % ny
                    pairs.append((src, dst))
            cells.append(lax.ppermute(rounded, ("gx", "gy"), pairs))
    return cells


def apply_kernel(src_ref, dst_ref, coef_ref, *refs):
    cells = refs[:9]
    cur_ref, prev_ref, cpl_hbm = refs[9:12]
    out_ref, out_bf_ref = refs[12:14]
    win, cpl, acc, sems = refs[14:]
    slots = cpl.shape[0]
    chunks = slots // CHUNK
    depth = cur_ref.shape[0]

    copies = []
    for c in range(chunks):
        cp = pltpu.make_async_copy(
            cpl_hbm.at[pl.ds(c * CHUNK, CHUNK)], cpl.at[pl.ds(c * CHUNK, CHUNK)], sems.at[c]
        )
        cp.start()
        copies.append(cp)

    for c in range(9):
        win[pl.ds(c * depth, depth)] = cells[c][...]
    acc[...] = jnp.zeros_like(acc)

    for c in range(chunks):
        copies[c].wait()

        def body(i, carry, c=c):
            s = c * CHUNK + i
            y = win[src_ref[s]]
            prod = lax.dot_general(
                y, cpl[s], (((1,), (1,)), ((), ())), preferred_element_type=jnp.float32
            )
            t = dst_ref[s]
            acc[t] = acc[t] + prod
            return carry

        lax.fori_loop(0, CHUNK, body, 0)

    alpha = coef_ref[0]
    beta = coef_ref[1]
    for z in range(depth):
        cur = cur_ref[z]
        nxt = alpha * (acc[z] - CENTER * cur) - beta * prev_ref[z]
        out_ref[z] = nxt
        out_bf_ref[z] = nxt.astype(jnp.bfloat16)


def apply_step(cells, cur, prev, matrices, sources, targets, coef):
    depth, vectors, dof = cur.shape
    slots = matrices.shape[0]
    vmem = pltpu.MemorySpace.VMEM
    smem = pltpu.MemorySpace.SMEM
    in_specs = (
        [pl.BlockSpec(memory_space=smem)] * 3
        + [pl.BlockSpec(memory_space=vmem)] * 11
        + [pl.BlockSpec(memory_space=pl.ANY)]
    )
    flops = 2 * slots * vectors * dof * dof
    bytes_accessed = slots * dof * dof * 2 + 9 * cur.size * 2 + 4 * cur.size * 4
    return pl.pallas_call(
        apply_kernel,
        out_shape=(
            jax.ShapeDtypeStruct(cur.shape, jnp.float32),
            jax.ShapeDtypeStruct(cur.shape, jnp.bfloat16),
        ),
        in_specs=in_specs,
        out_specs=(pl.BlockSpec(memory_space=vmem), pl.BlockSpec(memory_space=vmem)),
        scratch_shapes=[
            pltpu.VMEM((9 * depth, vectors, dof), jnp.bfloat16),
            pltpu.VMEM((slots, dof, dof), jnp.bfloat16),
            pltpu.VMEM((depth + 1, vectors, dof), jnp.float32),
            pltpu.SemaphoreType.DMA((slots // CHUNK,)),
        ],
        cost_estimate=pl.CostEstimate(flops=flops, bytes_accessed=bytes_accessed, transcendentals=0),
        compiler_params=pltpu.CompilerParams(vmem_limit_bytes=32 * 1024 * 1024),
    )(sources, targets, coef, *cells, cur, prev, matrices)


def orthonormal(filtered, rows_total):
    partial_gram = jnp.einsum(
        "zvd,zwd->vw", filtered, filtered, precision=lax.Precision.HIGHEST
    )
    gram_matrix = lax.psum(partial_gram, ("gx", "gy"))
    factor = jnp.linalg.cholesky(gram_matrix)
    identity = jnp.eye(filtered.shape[1], dtype=jnp.float32)
    inverse = jax.scipy.linalg.solve_triangular(factor, identity, lower=True)
    result = jnp.einsum("vw,zwd->zvd", inverse, filtered, precision=lax.Precision.HIGHEST)
    return result * math.sqrt(rows_total)


def local(basis, coupling, cpl_dst, cpl_src):
    column_depth = basis.shape[2]
    block_rows = basis.shape[4]
    matrices = coupling[0, 0]
    targets = cpl_dst[0, 0]
    sources = cpl_src[0, 0]
    rows_total = lax.axis_size("gx") * lax.axis_size("gy") * column_depth * block_rows

    def coefs(alpha, beta):
        return jnp.array([alpha, beta], dtype=jnp.float32)

    sigma_one = HALF / (LOWEST - CENTER)
    current = basis[0, 0]
    for outer in range(STEPS):
        previous = current
        rounded = current.astype(jnp.bfloat16)
        cells = gather_window(rounded)
        current, rounded = apply_step(
            cells, current, previous, matrices, sources, targets,
            coefs(sigma_one / HALF, 0.0),
        )
        sigma_now = sigma_one
        for inner in range(1, DEGREE):
            sigma_next = 1.0 / (2.0 / sigma_one - sigma_now)
            cells = gather_window(rounded)
            following, rounded = apply_step(
                cells, current, previous, matrices, sources, targets,
                coefs(2.0 * sigma_next / HALF, sigma_now * sigma_next),
            )
            previous, current, sigma_now = (current, following, sigma_next)
        current = orthonormal(current, rows_total)
    return current[None, None]


def solution(mesh):
    placed = (
        P("gx", "gy", None, None, None),
        P("gx", "gy", None, None, None),
        P("gx", "gy", None),
        P("gx", "gy", None),
    )
    return jax.shard_map(
        local,
        mesh=mesh,
        in_specs=placed,
        out_specs=P("gx", "gy", None, None, None),
        check_vma=False,
    )
```

```python
import math

import jax
import jax.numpy as jnp
from jax import lax
from jax.sharding import PartitionSpec as P

DEGREE = 8
STEPS = 2


CENTER = 5.0
HALF = 3.0
LOWEST = 0.5


def with_halo(cells, sides, width):
    for axis, dim in sides:
        count = lax.axis_size(axis)
        head = lax.slice_in_dim(cells, 0, width, axis=dim)
        tail = lax.slice_in_dim(cells, cells.shape[dim] - width, cells.shape[dim], axis=dim)
        cells = jnp.concatenate(
            [
                lax.ppermute(tail, axis, [(i, (i + 1) % count) for i in range(count)]),
                cells,
                lax.ppermute(head, axis, [((i + 1) % count, i) for i in range(count)]),
            ],
            axis=dim,
        )
    return cells


def dense_coupling(matrices, targets, sources, depth, cells):
    slots = matrices.shape[0]
    match = (targets[:, None, None] == jnp.arange(depth, dtype=jnp.int32)[None, :, None]) & (
        sources[:, None, None] == jnp.arange(cells, dtype=jnp.int32)[None, None, :]
    )
    slot_ids = jnp.arange(slots, dtype=jnp.int32)[:, None, None]
    index = jnp.sum(jnp.where(match, slot_ids, 0), axis=0)
    present = jnp.any(match, axis=0)
    blocks = jnp.take(matrices, index.reshape(-1), axis=0).reshape(
        depth, cells, matrices.shape[1], matrices.shape[2]
    )
    blocks = jnp.where(present[:, :, None, None], blocks, jnp.zeros((), matrices.dtype))
    return jnp.transpose(blocks, (0, 2, 1, 3))


def orthonormal(filtered, rows_total):
    partial_gram = jnp.einsum(
        "zvd,zwd->vw", filtered, filtered, precision=lax.Precision.HIGHEST
    )
    gram_matrix = lax.psum(partial_gram, ("gx", "gy"))
    factor = jnp.linalg.cholesky(gram_matrix)
    identity = jnp.eye(filtered.shape[1], dtype=jnp.float32)
    inverse = jax.scipy.linalg.solve_triangular(factor, identity, lower=True)
    result = jnp.einsum("vw,zwd->zvd", inverse, filtered, precision=lax.Precision.HIGHEST)
    return result * math.sqrt(rows_total)


def local(basis, coupling, cpl_dst, cpl_src):
    column_depth = basis.shape[2]
    vector_count = basis.shape[3]
    block_rows = basis.shape[4]
    rows_total = lax.axis_size("gx") * lax.axis_size("gy") * column_depth * block_rows
    dense = dense_coupling(coupling[0, 0], cpl_dst[0, 0], cpl_src[0, 0], column_depth, 9 * column_depth)

    def apply_operator(current):
        rounded = current.astype(jnp.bfloat16)[None, None]
        window = with_halo(rounded, (("gx", 0), ("gy", 1)), 1)
        window_cells = window.reshape(9 * column_depth, vector_count, block_rows)
        return jnp.einsum("kvj,tikj->tvi", window_cells, dense, preferred_element_type=jnp.float32)

    sigma_one = HALF / (LOWEST - CENTER)
    current_basis = basis[0, 0]
    for outer in range(STEPS):
        previous = current_basis
        current = sigma_one / HALF * (apply_operator(previous) - CENTER * previous)
        sigma_now = sigma_one
        for inner in range(1, DEGREE):
            sigma_next = 1.0 / (2.0 / sigma_one - sigma_now)
            image = apply_operator(current)
            following = (
                2.0 * sigma_next / HALF * (image - CENTER * current)
                - sigma_now * sigma_next * previous
            )
            previous, current, sigma_now = (current, following, sigma_next)
        current_basis = orthonormal(current, rows_total)
    return current_basis[None, None]


def solution(mesh):
    placed = (
        P("gx", "gy", None, None, None),
        P("gx", "gy", None, None, None),
        P("gx", "gy", None),
        P("gx", "gy", None),
    )
    return jax.shard_map(
        local,
        mesh=mesh,
        in_specs=placed,
        out_specs=P("gx", "gy", None, None, None),
        check_vma=False,
    )
```

```python
import math

import jax
import jax.numpy as jnp
from jax import lax
from jax.sharding import PartitionSpec as P

DEGREE = 8
STEPS = 2


CENTER = 5.0
HALF = 3.0
LOWEST = 0.5


def with_halo(cells, sides, width):
    for axis, dim in sides:
        count = lax.axis_size(axis)
        head = lax.slice_in_dim(cells, 0, width, axis=dim)
        tail = lax.slice_in_dim(cells, cells.shape[dim] - width, cells.shape[dim], axis=dim)
        cells = jnp.concatenate(
            [
                lax.ppermute(tail, axis, [(i, (i + 1) % count) for i in range(count)]),
                cells,
                lax.ppermute(head, axis, [((i + 1) % count, i) for i in range(count)]),
            ],
            axis=dim,
        )
    return cells


def dense_coupling(matrices, targets, sources, depth, cells):
    slots = matrices.shape[0]
    match = (targets[:, None, None] == jnp.arange(depth, dtype=jnp.int32)[None, :, None]) & (
        sources[:, None, None] == jnp.arange(cells, dtype=jnp.int32)[None, None, :]
    )
    slot_ids = jnp.arange(slots, dtype=jnp.int32)[:, None, None]
    index = jnp.sum(jnp.where(match, slot_ids, 0), axis=0)
    present = jnp.any(match, axis=0)
    blocks = jnp.take(matrices, index.reshape(-1), axis=0).reshape(
        depth, cells, matrices.shape[1], matrices.shape[2]
    )
    blocks = jnp.where(present[:, :, None, None], blocks, jnp.zeros((), matrices.dtype))
    return jnp.transpose(blocks, (0, 2, 1, 3))


def all_sum(value, axes):
    for axis in axes:
        count = lax.axis_size(axis)
        if count & (count - 1):
            value = lax.psum(value, axis)
            continue
        stride = 1
        while stride < count:
            value = value + lax.ppermute(value, axis, [(i, i ^ stride) for i in range(count)])
            stride *= 2
    return value


def orthonormal(filtered, rows_total):
    partial_gram = jnp.einsum(
        "zvd,zwd->vw", filtered, filtered, precision=lax.Precision.HIGHEST
    )
    gram_matrix = all_sum(partial_gram, ("gx", "gy"))
    factor = jnp.linalg.cholesky(gram_matrix)
    identity = jnp.eye(filtered.shape[1], dtype=jnp.float32)
    inverse = jax.scipy.linalg.solve_triangular(factor, identity, lower=True)
    result = jnp.einsum("vw,zwd->zvd", inverse, filtered, precision=lax.Precision.HIGHEST)
    return result * math.sqrt(rows_total)


def local(basis, coupling, cpl_dst, cpl_src):
    column_depth = basis.shape[2]
    vector_count = basis.shape[3]
    block_rows = basis.shape[4]
    rows_total = lax.axis_size("gx") * lax.axis_size("gy") * column_depth * block_rows
    dense = dense_coupling(coupling[0, 0], cpl_dst[0, 0], cpl_src[0, 0], column_depth, 9 * column_depth)

    def apply_operator(current):
        rounded = current.astype(jnp.bfloat16)[None, None]
        window = with_halo(rounded, (("gx", 0), ("gy", 1)), 1)
        window_cells = window.reshape(9 * column_depth, vector_count, block_rows)
        return jnp.einsum("kvj,tikj->tvi", window_cells, dense, preferred_element_type=jnp.float32)

    sigma_one = HALF / (LOWEST - CENTER)
    current_basis = basis[0, 0]
    for outer in range(STEPS):
        previous = current_basis
        current = sigma_one / HALF * (apply_operator(previous) - CENTER * previous)
        sigma_now = sigma_one
        for inner in range(1, DEGREE):
            sigma_next = 1.0 / (2.0 / sigma_one - sigma_now)
            image = apply_operator(current)
            following = (
                2.0 * sigma_next / HALF * (image - CENTER * current)
                - sigma_now * sigma_next * previous
            )
            previous, current, sigma_now = (current, following, sigma_next)
        current_basis = orthonormal(current, rows_total)
    return current_basis[None, None]


def solution(mesh):
    placed = (
        P("gx", "gy", None, None, None),
        P("gx", "gy", None, None, None),
        P("gx", "gy", None),
        P("gx", "gy", None),
    )
    return jax.shard_map(
        local,
        mesh=mesh,
        in_specs=placed,
        out_specs=P("gx", "gy", None, None, None),
        check_vma=False,
    )
```

```python
import math

import jax
import jax.numpy as jnp
from jax import lax
from jax.sharding import PartitionSpec as P

DEGREE = 8
STEPS = 2


CENTER = 5.0
HALF = 3.0
LOWEST = 0.5


def with_halo(cells, sides, width):
    for axis, dim in sides:
        count = lax.axis_size(axis)
        head = lax.slice_in_dim(cells, 0, width, axis=dim)
        tail = lax.slice_in_dim(cells, cells.shape[dim] - width, cells.shape[dim], axis=dim)
        cells = jnp.concatenate(
            [
                lax.ppermute(tail, axis, [(i, (i + 1) % count) for i in range(count)]),
                cells,
                lax.ppermute(head, axis, [((i + 1) % count, i) for i in range(count)]),
            ],
            axis=dim,
        )
    return cells


def dense_coupling(matrices, targets, sources, depth, order):
    slots = matrices.shape[0]
    cells = len(order)
    match = (targets[:, None, None] == jnp.arange(depth, dtype=jnp.int32)[None, :, None]) & (
        sources[:, None, None] == jnp.array(order, dtype=jnp.int32)[None, None, :]
    )
    slot_ids = jnp.arange(slots, dtype=jnp.int32)[:, None, None]
    index = jnp.sum(jnp.where(match, slot_ids, 0), axis=0)
    present = jnp.any(match, axis=0)
    blocks = jnp.take(matrices, index.reshape(-1), axis=0).reshape(
        depth, cells, matrices.shape[1], matrices.shape[2]
    )
    blocks = jnp.where(present[:, :, None, None], blocks, jnp.zeros((), matrices.dtype))
    return jnp.transpose(blocks, (0, 2, 1, 3))


def all_sum(value, axes):
    for axis in axes:
        count = lax.axis_size(axis)
        if count & (count - 1):
            value = lax.psum(value, axis)
            continue
        stride = 1
        while stride < count:
            value = value + lax.ppermute(value, axis, [(i, i ^ stride) for i in range(count)])
            stride *= 2
    return value


def orthonormal(filtered, rows_total):
    partial_gram = jnp.einsum(
        "zvd,zwd->vw", filtered, filtered, precision=lax.Precision.HIGHEST
    )
    gram_matrix = all_sum(partial_gram, ("gx", "gy"))
    factor = jnp.linalg.cholesky(gram_matrix)
    identity = jnp.eye(filtered.shape[1], dtype=jnp.float32)
    inverse = jax.scipy.linalg.solve_triangular(factor, identity, lower=True)
    result = jnp.einsum("vw,zwd->zvd", inverse, filtered, precision=lax.Precision.HIGHEST)
    return result * math.sqrt(rows_total)


def local(basis, coupling, cpl_dst, cpl_src):
    column_depth = basis.shape[2]
    vector_count = basis.shape[3]
    block_rows = basis.shape[4]
    rows_total = lax.axis_size("gx") * lax.axis_size("gy") * column_depth * block_rows
    columns = [(1, 1), (0, 1), (2, 1)] + [(dx, 0) for dx in range(3)] + [(dx, 2) for dx in range(3)]
    order = [(3 * dx + dy) * column_depth + z for dx, dy in columns for z in range(column_depth)]
    dense = dense_coupling(coupling[0, 0], cpl_dst[0, 0], cpl_src[0, 0], column_depth, order)
    dense_own = dense[:, :, :column_depth]
    dense_side = dense[:, :, column_depth:3 * column_depth]
    dense_far = dense[:, :, 3 * column_depth:]

    def shift(value, axis, step):
        count = lax.axis_size(axis)
        return lax.ppermute(value, axis, [(i, (i + step) % count) for i in range(count)])

    def part(cells, blocks):
        return jnp.einsum("kvj,tikj->tvi", cells, blocks, preferred_element_type=jnp.float32)

    def apply_operator(current):
        rounded = current.astype(jnp.bfloat16)
        left = shift(rounded, "gx", 1)
        right = shift(rounded, "gx", -1)
        image = part(rounded, dense_own)
        strip = jnp.stack([left, rounded, right])
        low = shift(strip, "gy", 1)
        high = shift(strip, "gy", -1)
        image = image + part(jnp.concatenate([left, right]), dense_side)
        far = jnp.concatenate([low, high]).reshape(6 * column_depth, vector_count, block_rows)
        return image + part(far, dense_far)

    sigma_one = HALF / (LOWEST - CENTER)
    current_basis = basis[0, 0]
    for outer in range(STEPS):
        previous = current_basis
        current = sigma_one / HALF * (apply_operator(previous) - CENTER * previous)
        sigma_now = sigma_one
        for inner in range(1, DEGREE):
            sigma_next = 1.0 / (2.0 / sigma_one - sigma_now)
            image = apply_operator(current)
            following = (
                2.0 * sigma_next / HALF * (image - CENTER * current)
                - sigma_now * sigma_next * previous
            )
            previous, current, sigma_now = (current, following, sigma_next)
        current_basis = orthonormal(current, rows_total)
    return current_basis[None, None]


def solution(mesh):
    placed = (
        P("gx", "gy", None, None, None),
        P("gx", "gy", None, None, None),
        P("gx", "gy", None),
        P("gx", "gy", None),
    )
    return jax.shard_map(
        local,
        mesh=mesh,
        in_specs=placed,
        out_specs=P("gx", "gy", None, None, None),
        check_vma=False,
    )
```

```python
import math

import jax
import jax.numpy as jnp
from jax import lax
from jax.sharding import PartitionSpec as P

DEGREE = 8
STEPS = 2


CENTER = 5.0
HALF = 3.0
LOWEST = 0.5


def with_halo(cells, sides, width):
    for axis, dim in sides:
        count = lax.axis_size(axis)
        head = lax.slice_in_dim(cells, 0, width, axis=dim)
        tail = lax.slice_in_dim(cells, cells.shape[dim] - width, cells.shape[dim], axis=dim)
        cells = jnp.concatenate(
            [
                lax.ppermute(tail, axis, [(i, (i + 1) % count) for i in range(count)]),
                cells,
                lax.ppermute(head, axis, [((i + 1) % count, i) for i in range(count)]),
            ],
            axis=dim,
        )
    return cells


def dense_coupling(matrices, targets, sources, depth, order):
    slots = matrices.shape[0]
    cells = len(order)
    match = (targets[:, None, None] == jnp.arange(depth, dtype=jnp.int32)[None, :, None]) & (
        sources[:, None, None] == jnp.array(order, dtype=jnp.int32)[None, None, :]
    )
    select = match.reshape(slots, depth * cells).astype(matrices.dtype)
    blocks = jnp.einsum("sc,sij->cij", select, matrices, preferred_element_type=jnp.float32)
    return blocks.astype(matrices.dtype).reshape(depth, cells, matrices.shape[1], matrices.shape[2])


def all_sum(value, axes):
    for axis in axes:
        count = lax.axis_size(axis)
        if count & (count - 1):
            value = lax.psum(value, axis)
            continue
        stride = 1
        while stride < count:
            value = value + lax.ppermute(value, axis, [(i, i ^ stride) for i in range(count)])
            stride *= 2
    return value


def orthonormal(filtered, rows_total):
    partial_gram = jnp.einsum(
        "zvd,zwd->vw", filtered, filtered, precision=lax.Precision.HIGHEST
    )
    gram_matrix = all_sum(partial_gram, ("gx", "gy"))
    factor = jnp.linalg.cholesky(gram_matrix)
    identity = jnp.eye(filtered.shape[1], dtype=jnp.float32)
    inverse = jax.scipy.linalg.solve_triangular(factor, identity, lower=True)
    result = jnp.einsum("vw,zwd->zvd", inverse, filtered, precision=lax.Precision.HIGHEST)
    return result * math.sqrt(rows_total)


def local(basis, coupling, cpl_dst, cpl_src):
    column_depth = basis.shape[2]
    vector_count = basis.shape[3]
    block_rows = basis.shape[4]
    rows_total = lax.axis_size("gx") * lax.axis_size("gy") * column_depth * block_rows
    columns = [(1, 1), (0, 1), (2, 1)] + [(dx, 0) for dx in range(3)] + [(dx, 2) for dx in range(3)]
    order = [(3 * dx + dy) * column_depth + z for dx, dy in columns for z in range(column_depth)]
    dense = dense_coupling(coupling[0, 0], cpl_dst[0, 0], cpl_src[0, 0], column_depth, order)
    dense_own = dense[:, :column_depth]
    dense_side = dense[:, column_depth:3 * column_depth]
    dense_low = dense[:, 3 * column_depth:6 * column_depth]
    dense_high = dense[:, 6 * column_depth:]

    def shift(value, axis, step):
        count = lax.axis_size(axis)
        return lax.ppermute(value, axis, [(i, (i + step) % count) for i in range(count)])

    def part(cells, blocks):
        return jnp.einsum("kvj,tkij->tvi", cells, blocks, preferred_element_type=jnp.float32)

    def apply_operator(current):
        rounded = current.astype(jnp.bfloat16)
        left = shift(rounded, "gx", 1)
        right = shift(rounded, "gx", -1)
        image = part(rounded, dense_own)
        strip = jnp.stack([left, rounded, right])
        low = shift(strip, "gy", 1)
        high = shift(strip, "gy", -1)
        image = image + part(jnp.concatenate([left, right]), dense_side)
        image = image + part(low.reshape(3 * column_depth, vector_count, block_rows), dense_low)
        return image + part(high.reshape(3 * column_depth, vector_count, block_rows), dense_high)

    sigma_one = HALF / (LOWEST - CENTER)
    current_basis = basis[0, 0]
    for outer in range(STEPS):
        previous = current_basis
        current = sigma_one / HALF * (apply_operator(previous) - CENTER * previous)
        sigma_now = sigma_one
        for inner in range(1, DEGREE):
            sigma_next = 1.0 / (2.0 / sigma_one - sigma_now)
            image = apply_operator(current)
            following = (
                2.0 * sigma_next / HALF * (image - CENTER * current)
                - sigma_now * sigma_next * previous
            )
            previous, current, sigma_now = (current, following, sigma_next)
        current_basis = orthonormal(current, rows_total)
    return current_basis[None, None]


def solution(mesh):
    placed = (
        P("gx", "gy", None, None, None),
        P("gx", "gy", None, None, None),
        P("gx", "gy", None),
        P("gx", "gy", None),
    )
    return jax.shard_map(
        local,
        mesh=mesh,
        in_specs=placed,
        out_specs=P("gx", "gy", None, None, None),
        check_vma=False,
    )
```

```python
import math

import jax
import jax.numpy as jnp
from jax import lax
from jax.sharding import PartitionSpec as P

DEGREE = 8
STEPS = 2


CENTER = 5.0
HALF = 3.0
LOWEST = 0.5


def with_halo(cells, sides, width):
    for axis, dim in sides:
        count = lax.axis_size(axis)
        head = lax.slice_in_dim(cells, 0, width, axis=dim)
        tail = lax.slice_in_dim(cells, cells.shape[dim] - width, cells.shape[dim], axis=dim)
        cells = jnp.concatenate(
            [
                lax.ppermute(tail, axis, [(i, (i + 1) % count) for i in range(count)]),
                cells,
                lax.ppermute(head, axis, [((i + 1) % count, i) for i in range(count)]),
            ],
            axis=dim,
        )
    return cells


def dense_coupling(matrices, targets, sources, depth, order):
    slots = matrices.shape[0]
    cells = len(order)
    match = (targets[:, None, None] == jnp.arange(depth, dtype=jnp.int32)[None, :, None]) & (
        sources[:, None, None] == jnp.array(order, dtype=jnp.int32)[None, None, :]
    )
    slot_ids = jnp.arange(slots, dtype=jnp.int32)[:, None, None]
    index = jnp.sum(jnp.where(match, slot_ids, 0), axis=0)
    present = jnp.any(match, axis=0)
    blocks = jnp.take(matrices, index.reshape(-1), axis=0).reshape(
        depth, cells, matrices.shape[1], matrices.shape[2]
    )
    return jnp.where(present[:, :, None, None], blocks, jnp.zeros((), matrices.dtype))


def all_sum(value, axes):
    for axis in axes:
        count = lax.axis_size(axis)
        if count & (count - 1):
            value = lax.psum(value, axis)
            continue
        stride = 1
        while stride < count:
            value = value + lax.ppermute(value, axis, [(i, i ^ stride) for i in range(count)])
            stride *= 2
    return value


def orthonormal_scale(filtered, rows_total):
    partial_gram = jnp.einsum(
        "zvd,zwd->vw", filtered, filtered, precision=lax.Precision.HIGHEST
    )
    gram_matrix = all_sum(partial_gram, ("gx", "gy"))
    factor = jnp.linalg.cholesky(gram_matrix)
    identity = jnp.eye(filtered.shape[1], dtype=jnp.float32)
    inverse = jax.scipy.linalg.solve_triangular(factor, identity, lower=True)
    return inverse, math.sqrt(rows_total)


def normalize(scale, filtered):
    inverse, factor = scale
    shape = filtered.shape
    cells = filtered.reshape((-1,) + shape[-2:])
    result = jnp.einsum("vw,zwd->zvd", inverse, cells, precision=lax.Precision.HIGHEST)
    return (result * factor).reshape(shape)


def local(basis, coupling, cpl_dst, cpl_src):
    column_depth = basis.shape[2]
    vector_count = basis.shape[3]
    block_rows = basis.shape[4]
    rows_total = lax.axis_size("gx") * lax.axis_size("gy") * column_depth * block_rows
    columns = [(1, 1), (0, 1), (2, 1)] + [(dx, 0) for dx in range(3)] + [(dx, 2) for dx in range(3)]
    order = [(3 * dx + dy) * column_depth + z for dx, dy in columns for z in range(column_depth)]
    def build(first, last):
        return dense_coupling(coupling[0, 0], cpl_dst[0, 0], cpl_src[0, 0], column_depth,
                              order[first * column_depth:last * column_depth])

    dense_own = build(0, 1)
    dense_side = build(1, 3)
    dense_low = build(3, 6)
    dense_high = build(6, 9)

    def shift(value, axis, step):
        count = lax.axis_size(axis)
        return lax.ppermute(value, axis, [(i, (i + step) % count) for i in range(count)])

    def part(cells, blocks):
        return jnp.einsum("kvj,tkij->tvi", cells, blocks, preferred_element_type=jnp.float32)

    def apply_cells(own, left, right, low, high):
        image = part(own, dense_own)
        image = image + part(jnp.concatenate([left, right]), dense_side)
        image = image + part(low.reshape(3 * column_depth, vector_count, block_rows), dense_low)
        return image + part(high.reshape(3 * column_depth, vector_count, block_rows), dense_high)

    def halo(own):
        left = shift(own, "gx", 1)
        right = shift(own, "gx", -1)
        strip = jnp.stack([left, own, right])
        return left, right, shift(strip, "gy", 1), shift(strip, "gy", -1)

    def apply_operator(current):
        rounded = current.astype(jnp.bfloat16)
        return apply_cells(rounded, *halo(rounded))

    sigma_one = HALF / (LOWEST - CENTER)
    current_basis = basis[0, 0]
    image = apply_operator(current_basis)
    for outer in range(STEPS):
        previous = current_basis
        current = sigma_one / HALF * (image - CENTER * previous)
        sigma_now = sigma_one
        for inner in range(1, DEGREE):
            sigma_next = 1.0 / (2.0 / sigma_one - sigma_now)
            image = apply_operator(current)
            following = (
                2.0 * sigma_next / HALF * (image - CENTER * current)
                - sigma_now * sigma_next * previous
            )
            previous, current, sigma_now = (current, following, sigma_next)
        if outer + 1 < STEPS:
            filtered_halo = halo(current)
            scale = orthonormal_scale(current, rows_total)
            current_basis = normalize(scale, current)
            cells = [normalize(scale, cell).astype(jnp.bfloat16) for cell in filtered_halo]
            image = apply_cells(current_basis.astype(jnp.bfloat16), *cells)
        else:
            current_basis = normalize(orthonormal_scale(current, rows_total), current)
    return current_basis[None, None]


def solution(mesh):
    placed = (
        P("gx", "gy", None, None, None),
        P("gx", "gy", None, None, None),
        P("gx", "gy", None),
        P("gx", "gy", None),
    )
    return jax.shard_map(
        local,
        mesh=mesh,
        in_specs=placed,
        out_specs=P("gx", "gy", None, None, None),
        check_vma=False,
    )
```

```python
import math

import jax
import jax.numpy as jnp
from jax import lax
from jax.sharding import PartitionSpec as P

DEGREE = 8
STEPS = 2


CENTER = 5.0
HALF = 3.0
LOWEST = 0.5


def with_halo(cells, sides, width):
    for axis, dim in sides:
        count = lax.axis_size(axis)
        head = lax.slice_in_dim(cells, 0, width, axis=dim)
        tail = lax.slice_in_dim(cells, cells.shape[dim] - width, cells.shape[dim], axis=dim)
        cells = jnp.concatenate(
            [
                lax.ppermute(tail, axis, [(i, (i + 1) % count) for i in range(count)]),
                cells,
                lax.ppermute(head, axis, [((i + 1) % count, i) for i in range(count)]),
            ],
            axis=dim,
        )
    return cells


def dense_coupling(matrices, targets, sources, depth, order):
    slots = matrices.shape[0]
    cells = len(order)
    match = (targets[:, None, None] == jnp.arange(depth, dtype=jnp.int32)[None, :, None]) & (
        sources[:, None, None] == jnp.array(order, dtype=jnp.int32)[None, None, :]
    )
    slot_ids = jnp.arange(slots, dtype=jnp.int32)[:, None, None]
    index = jnp.sum(jnp.where(match, slot_ids, 0), axis=0)
    present = jnp.any(match, axis=0)
    blocks = jnp.take(matrices, index.reshape(-1), axis=0).reshape(
        depth, cells, matrices.shape[1], matrices.shape[2]
    )
    return lax.optimization_barrier(
        jnp.where(present[:, :, None, None], blocks, jnp.zeros((), matrices.dtype))
    )


def all_sum(value, axes):
    for axis in axes:
        count = lax.axis_size(axis)
        if count & (count - 1):
            value = lax.psum(value, axis)
            continue
        stride = 1
        while stride < count:
            value = value + lax.ppermute(value, axis, [(i, i ^ stride) for i in range(count)])
            stride *= 2
    return value


def orthonormal(filtered, rows_total):
    partial_gram = jnp.einsum(
        "zvd,zwd->vw", filtered, filtered, precision=lax.Precision.HIGHEST
    )
    gram_matrix = all_sum(partial_gram, ("gx", "gy"))
    factor = jnp.linalg.cholesky(gram_matrix)
    identity = jnp.eye(filtered.shape[1], dtype=jnp.float32)
    inverse = jax.scipy.linalg.solve_triangular(factor, identity, lower=True)
    result = jnp.einsum("vw,zwd->zvd", inverse, filtered, precision=lax.Precision.HIGHEST)
    return result * math.sqrt(rows_total)


def local(basis, coupling, cpl_dst, cpl_src):
    column_depth = basis.shape[2]
    vector_count = basis.shape[3]
    block_rows = basis.shape[4]
    rows_total = lax.axis_size("gx") * lax.axis_size("gy") * column_depth * block_rows
    columns = [(1, 1), (0, 1), (2, 1)] + [(dx, 0) for dx in range(3)] + [(dx, 2) for dx in range(3)]
    order = [(3 * dx + dy) * column_depth + z for dx, dy in columns for z in range(column_depth)]
    dense = dense_coupling(coupling[0, 0], cpl_dst[0, 0], cpl_src[0, 0], column_depth, order)
    dense_own = dense[:, :column_depth]
    dense_side = dense[:, column_depth:3 * column_depth]
    dense_low = dense[:, 3 * column_depth:6 * column_depth]
    dense_high = dense[:, 6 * column_depth:]

    def shift(value, axis, step):
        count = lax.axis_size(axis)
        return lax.ppermute(value, axis, [(i, (i + step) % count) for i in range(count)])

    def part(cells, blocks):
        return jnp.einsum("kvj,tkij->tvi", cells, blocks, preferred_element_type=jnp.float32)

    def apply_operator(current):
        rounded = current.astype(jnp.bfloat16)
        left = shift(rounded, "gx", 1)
        right = shift(rounded, "gx", -1)
        image = part(rounded, dense_own)
        strip = jnp.stack([left, rounded, right])
        low = shift(strip, "gy", 1)
        high = shift(strip, "gy", -1)
        image = image + part(jnp.concatenate([left, right]), dense_side)
        image = image + part(low.reshape(3 * column_depth, vector_count, block_rows), dense_low)
        return image + part(high.reshape(3 * column_depth, vector_count, block_rows), dense_high)

    sigma_one = HALF / (LOWEST - CENTER)
    current_basis = basis[0, 0]
    for outer in range(STEPS):
        previous = current_basis
        current = sigma_one / HALF * (apply_operator(previous) - CENTER * previous)
        sigma_now = sigma_one
        for inner in range(1, DEGREE):
            sigma_next = 1.0 / (2.0 / sigma_one - sigma_now)
            image = apply_operator(current)
            following = (
                2.0 * sigma_next / HALF * (image - CENTER * current)
                - sigma_now * sigma_next * previous
            )
            previous, current, sigma_now = (current, following, sigma_next)
        current_basis = orthonormal(current, rows_total)
    return current_basis[None, None]


def solution(mesh):
    placed = (
        P("gx", "gy", None, None, None),
        P("gx", "gy", None, None, None),
        P("gx", "gy", None),
        P("gx", "gy", None),
    )
    return jax.shard_map(
        local,
        mesh=mesh,
        in_specs=placed,
        out_specs=P("gx", "gy", None, None, None),
        check_vma=False,
    )
```

```python
import math

import jax
import jax.numpy as jnp
from jax import lax
from jax.experimental import pallas as pl
from jax.experimental.pallas import tpu as pltpu
from jax.sharding import PartitionSpec as P

DEGREE = 8
STEPS = 2


CENTER = 5.0
HALF = 3.0
LOWEST = 0.5


def with_halo(cells, sides, width):
    for axis, dim in sides:
        count = lax.axis_size(axis)
        head = lax.slice_in_dim(cells, 0, width, axis=dim)
        tail = lax.slice_in_dim(cells, cells.shape[dim] - width, cells.shape[dim], axis=dim)
        cells = jnp.concatenate(
            [
                lax.ppermute(tail, axis, [(i, (i + 1) % count) for i in range(count)]),
                cells,
                lax.ppermute(head, axis, [((i + 1) % count, i) for i in range(count)]),
            ],
            axis=dim,
        )
    return cells


def gather_kernel(index_ref, present_ref, cpl_hbm, out_ref, zero, sems):
    zero[...] = jnp.zeros_like(zero)
    copies = []
    for c in range(out_ref.shape[0]):
        source = cpl_hbm.at[index_ref[c]]
        live = pltpu.make_async_copy(source, out_ref.at[c], sems.at[c])
        dead = pltpu.make_async_copy(zero, out_ref.at[c], sems.at[c])

        @pl.when(present_ref[c] != 0)
        def _():
            live.start()

        @pl.when(present_ref[c] == 0)
        def _():
            dead.start()

        copies.append(live)
    for cp in copies:
        cp.wait()


def dense_coupling(matrices, targets, sources, depth, order):
    slots, rows, cols = matrices.shape
    cells = len(order)
    match = (targets[:, None, None] == jnp.arange(depth, dtype=jnp.int32)[None, :, None]) & (
        sources[:, None, None] == jnp.array(order, dtype=jnp.int32)[None, None, :]
    )
    slot_ids = jnp.arange(slots, dtype=jnp.int32)[:, None, None]
    index = jnp.clip(jnp.sum(jnp.where(match, slot_ids, 0), axis=0), 0, slots - 1).reshape(-1)
    present = jnp.any(match, axis=0).astype(jnp.int32).reshape(-1)
    smem = pltpu.MemorySpace.SMEM
    blocks = pl.pallas_call(
        gather_kernel,
        out_shape=jax.ShapeDtypeStruct((depth * cells, rows, cols), matrices.dtype),
        in_specs=[
            pl.BlockSpec(memory_space=smem),
            pl.BlockSpec(memory_space=smem),
            pl.BlockSpec(memory_space=pl.ANY),
        ],
        out_specs=pl.BlockSpec(memory_space=pltpu.MemorySpace.VMEM),
        scratch_shapes=[
            pltpu.VMEM((rows, cols), matrices.dtype),
            pltpu.SemaphoreType.DMA((depth * cells,)),
        ],
        cost_estimate=pl.CostEstimate(
            flops=0, bytes_accessed=2 * depth * cells * rows * cols * 2, transcendentals=0
        ),
        compiler_params=pltpu.CompilerParams(vmem_limit_bytes=24 * 1024 * 1024),
    )(index, present, matrices)
    return blocks.reshape(depth, cells, rows, cols)


def all_sum(value, axes):
    for axis in axes:
        count = lax.axis_size(axis)
        if count & (count - 1):
            value = lax.psum(value, axis)
            continue
        stride = 1
        while stride < count:
            value = value + lax.ppermute(value, axis, [(i, i ^ stride) for i in range(count)])
            stride *= 2
    return value


def orthonormal(filtered, rows_total):
    partial_gram = jnp.einsum(
        "zvd,zwd->vw", filtered, filtered, precision=lax.Precision.HIGHEST
    )
    gram_matrix = all_sum(partial_gram, ("gx", "gy"))
    factor = jnp.linalg.cholesky(gram_matrix)
    identity = jnp.eye(filtered.shape[1], dtype=jnp.float32)
    inverse = jax.scipy.linalg.solve_triangular(factor, identity, lower=True)
    result = jnp.einsum("vw,zwd->zvd", inverse, filtered, precision=lax.Precision.HIGHEST)
    return result * math.sqrt(rows_total)


def local(basis, coupling, cpl_dst, cpl_src):
    column_depth = basis.shape[2]
    vector_count = basis.shape[3]
    block_rows = basis.shape[4]
    rows_total = lax.axis_size("gx") * lax.axis_size("gy") * column_depth * block_rows
    columns = [(1, 1), (0, 1), (2, 1)] + [(dx, 0) for dx in range(3)] + [(dx, 2) for dx in range(3)]
    order = [(3 * dx + dy) * column_depth + z for dx, dy in columns for z in range(column_depth)]
    dense = dense_coupling(coupling[0, 0], cpl_dst[0, 0], cpl_src[0, 0], column_depth, order)
    dense_own = dense[:, :column_depth]
    dense_side = dense[:, column_depth:3 * column_depth]
    dense_low = dense[:, 3 * column_depth:6 * column_depth]
    dense_high = dense[:, 6 * column_depth:]

    def shift(value, axis, step):
        count = lax.axis_size(axis)
        return lax.ppermute(value, axis, [(i, (i + step) % count) for i in range(count)])

    def part(cells, blocks):
        return jnp.einsum("kvj,tkij->tvi", cells, blocks, preferred_element_type=jnp.float32)

    def apply_operator(current):
        rounded = current.astype(jnp.bfloat16)
        left = shift(rounded, "gx", 1)
        right = shift(rounded, "gx", -1)
        image = part(rounded, dense_own)
        strip = jnp.stack([left, rounded, right])
        low = shift(strip, "gy", 1)
        high = shift(strip, "gy", -1)
        image = image + part(jnp.concatenate([left, right]), dense_side)
        image = image + part(low.reshape(3 * column_depth, vector_count, block_rows), dense_low)
        return image + part(high.reshape(3 * column_depth, vector_count, block_rows), dense_high)

    sigma_one = HALF / (LOWEST - CENTER)
    current_basis = basis[0, 0]
    for outer in range(STEPS):
        previous = current_basis
        current = sigma_one / HALF * (apply_operator(previous) - CENTER * previous)
        sigma_now = sigma_one
        for inner in range(1, DEGREE):
            sigma_next = 1.0 / (2.0 / sigma_one - sigma_now)
            image = apply_operator(current)
            following = (
                2.0 * sigma_next / HALF * (image - CENTER * current)
                - sigma_now * sigma_next * previous
            )
            previous, current, sigma_now = (current, following, sigma_next)
        current_basis = orthonormal(current, rows_total)
    return current_basis[None, None]


def solution(mesh):
    placed = (
        P("gx", "gy", None, None, None),
        P("gx", "gy", None, None, None),
        P("gx", "gy", None),
        P("gx", "gy", None),
    )
    return jax.shard_map(
        local,
        mesh=mesh,
        in_specs=placed,
        out_specs=P("gx", "gy", None, None, None),
        check_vma=False,
    )
```

```python
import math

import jax
import jax.numpy as jnp
from jax import lax
from jax.sharding import PartitionSpec as P

DEGREE = 8
STEPS = 2


CENTER = 5.0
HALF = 3.0
LOWEST = 0.5


def with_halo(cells, sides, width):
    for axis, dim in sides:
        count = lax.axis_size(axis)
        head = lax.slice_in_dim(cells, 0, width, axis=dim)
        tail = lax.slice_in_dim(cells, cells.shape[dim] - width, cells.shape[dim], axis=dim)
        cells = jnp.concatenate(
            [
                lax.ppermute(tail, axis, [(i, (i + 1) % count) for i in range(count)]),
                cells,
                lax.ppermute(head, axis, [((i + 1) % count, i) for i in range(count)]),
            ],
            axis=dim,
        )
    return cells


def dense_coupling(matrices, targets, sources, depth, order):
    slots = matrices.shape[0]
    cells = len(order)
    match = (targets[:, None, None] == jnp.arange(depth, dtype=jnp.int32)[None, :, None]) & (
        sources[:, None, None] == jnp.array(order, dtype=jnp.int32)[None, None, :]
    )
    slot_ids = jnp.arange(slots, dtype=jnp.int32)[:, None, None]
    index = jnp.sum(jnp.where(match, slot_ids, 0), axis=0)
    present = jnp.any(match, axis=0)
    blocks = jnp.take(matrices, index.reshape(-1), axis=0).reshape(
        depth, cells, matrices.shape[1], matrices.shape[2]
    )
    return lax.optimization_barrier(
        jnp.where(present[:, :, None, None], blocks, jnp.zeros((), matrices.dtype))
    )


def all_sum(value, axes):
    for axis in axes:
        count = lax.axis_size(axis)
        if count & (count - 1):
            value = lax.psum(value, axis)
            continue

        def swap(v, stride):
            return lax.ppermute(v, axis, [(i, i ^ stride) for i in range(count)])

        stride = 1
        while stride < count:
            if 4 * stride <= count:
                near, far, both = swap(value, stride), swap(value, 2 * stride), swap(value, 3 * stride)
                value = (value + near) + (far + both)
                stride *= 4
            else:
                value = value + swap(value, stride)
                stride *= 2
    return value


def orthonormal(filtered, rows_total):
    partial_gram = jnp.einsum(
        "zvd,zwd->vw", filtered, filtered, precision=lax.Precision.HIGHEST
    )
    gram_matrix = all_sum(partial_gram, ("gx", "gy"))
    factor = jnp.linalg.cholesky(gram_matrix)
    identity = jnp.eye(filtered.shape[1], dtype=jnp.float32)
    inverse = jax.scipy.linalg.solve_triangular(factor, identity, lower=True)
    result = jnp.einsum("vw,zwd->zvd", inverse, filtered, precision=lax.Precision.HIGHEST)
    return result * math.sqrt(rows_total)


def local(basis, coupling, cpl_dst, cpl_src):
    column_depth = basis.shape[2]
    vector_count = basis.shape[3]
    block_rows = basis.shape[4]
    rows_total = lax.axis_size("gx") * lax.axis_size("gy") * column_depth * block_rows
    columns = [(1, 1), (0, 1), (2, 1)] + [(dx, 0) for dx in range(3)] + [(dx, 2) for dx in range(3)]
    order = [(3 * dx + dy) * column_depth + z for dx, dy in columns for z in range(column_depth)]
    dense = dense_coupling(coupling[0, 0], cpl_dst[0, 0], cpl_src[0, 0], column_depth, order)
    dense_own = dense[:, :column_depth]
    dense_side = dense[:, column_depth:3 * column_depth]
    dense_low = dense[:, 3 * column_depth:6 * column_depth]
    dense_high = dense[:, 6 * column_depth:]

    def shift(value, axis, step):
        count = lax.axis_size(axis)
        return lax.ppermute(value, axis, [(i, (i + step) % count) for i in range(count)])

    def part(cells, blocks):
        return jnp.einsum("kvj,tkij->tvi", cells, blocks, preferred_element_type=jnp.float32)

    def apply_operator(current):
        rounded = current.astype(jnp.bfloat16)
        left = shift(rounded, "gx", 1)
        right = shift(rounded, "gx", -1)
        image = part(rounded, dense_own)
        strip = jnp.stack([left, rounded, right])
        low = shift(strip, "gy", 1)
        high = shift(strip, "gy", -1)
        image = image + part(jnp.concatenate([left, right]), dense_side)
        image = image + part(low.reshape(3 * column_depth, vector_count, block_rows), dense_low)
        return image + part(high.reshape(3 * column_depth, vector_count, block_rows), dense_high)

    sigma_one = HALF / (LOWEST - CENTER)
    current_basis = basis[0, 0]
    for outer in range(STEPS):
        previous = current_basis
        current = sigma_one / HALF * (apply_operator(previous) - CENTER * previous)
        sigma_now = sigma_one
        for inner in range(1, DEGREE):
            sigma_next = 1.0 / (2.0 / sigma_one - sigma_now)
            image = apply_operator(current)
            following = (
                2.0 * sigma_next / HALF * (image - CENTER * current)
                - sigma_now * sigma_next * previous
            )
            previous, current, sigma_now = (current, following, sigma_next)
        current_basis = orthonormal(current, rows_total)
    return current_basis[None, None]


def solution(mesh):
    placed = (
        P("gx", "gy", None, None, None),
        P("gx", "gy", None, None, None),
        P("gx", "gy", None),
        P("gx", "gy", None),
    )
    return jax.shard_map(
        local,
        mesh=mesh,
        in_specs=placed,
        out_specs=P("gx", "gy", None, None, None),
        check_vma=False,
    )
```

```python
import math

import jax
import jax.numpy as jnp
from jax import lax
from jax.experimental import pallas as pl
from jax.sharding import PartitionSpec as P

DEGREE = 8
STEPS = 2


CENTER = 5.0
HALF = 3.0
LOWEST = 0.5


def with_halo(cells, sides, width):
    for axis, dim in sides:
        count = lax.axis_size(axis)
        head = lax.slice_in_dim(cells, 0, width, axis=dim)
        tail = lax.slice_in_dim(cells, cells.shape[dim] - width, cells.shape[dim], axis=dim)
        cells = jnp.concatenate(
            [
                lax.ppermute(tail, axis, [(i, (i + 1) % count) for i in range(count)]),
                cells,
                lax.ppermute(head, axis, [((i + 1) % count, i) for i in range(count)]),
            ],
            axis=dim,
        )
    return cells


def dense_coupling(matrices, targets, sources, depth, order):
    slots = matrices.shape[0]
    cells = len(order)
    match = (targets[:, None, None] == jnp.arange(depth, dtype=jnp.int32)[None, :, None]) & (
        sources[:, None, None] == jnp.array(order, dtype=jnp.int32)[None, None, :]
    )
    slot_ids = jnp.arange(slots, dtype=jnp.int32)[:, None, None]
    index = jnp.sum(jnp.where(match, slot_ids, 0), axis=0)
    present = jnp.any(match, axis=0)
    blocks = jnp.take(matrices, index.reshape(-1), axis=0).reshape(
        depth, cells, matrices.shape[1], matrices.shape[2]
    )
    return lax.optimization_barrier(
        jnp.where(present[:, :, None, None], blocks, jnp.zeros((), matrices.dtype))
    )


def all_sum(value, axes):
    for axis in axes:
        count = lax.axis_size(axis)
        if count & (count - 1):
            value = lax.psum(value, axis)
            continue

        def swap(v, stride):
            return lax.ppermute(v, axis, [(i, i ^ stride) for i in range(count)])

        stride = 1
        while stride < count:
            if 4 * stride <= count:
                near, far, both = swap(value, stride), swap(value, 2 * stride), swap(value, 3 * stride)
                value = (value + near) + (far + both)
                stride *= 4
            else:
                value = value + swap(value, stride)
                stride *= 2
    return value


def chol_inv_kernel(g_ref, out_ref):
    a = g_ref[...]
    n = a.shape[0]
    rows = lax.broadcasted_iota(jnp.int32, (n, n), 0)
    lanes = lax.broadcasted_iota(jnp.int32, (n, n), 1)
    row_ids = lax.broadcasted_iota(jnp.int32, (n, 1), 0)
    lane_ids = lax.broadcasted_iota(jnp.int32, (1, n), 1)
    lower = jnp.zeros_like(a)
    upper = jnp.zeros_like(a)
    for j in range(n):
        col = jnp.sum(jnp.where(lanes == j, a, 0.0), axis=1, keepdims=True)
        row = jnp.sum(jnp.where(rows == j, a, 0.0), axis=0, keepdims=True)
        pivot = jnp.sqrt(jnp.sum(jnp.where(row_ids == j, col, 0.0), axis=0, keepdims=True))
        col = jnp.where(row_ids >= j, col / pivot, 0.0)
        row = jnp.where(lane_ids >= j, row / pivot, 0.0)
        lower = jnp.where(lanes == j, col, lower)
        upper = jnp.where(rows == j, row, upper)
        a = a - col * row
    inv = jnp.zeros_like(a)
    for i in range(n):
        coeff = jnp.sum(jnp.where(lanes == i, upper, 0.0), axis=1, keepdims=True)
        diag = jnp.sum(jnp.where(row_ids == i, coeff, 0.0), axis=0, keepdims=True)
        t = jnp.sum(coeff * inv, axis=0, keepdims=True)
        new = (jnp.where(lane_ids == i, 1.0, 0.0) - t) / diag
        inv = jnp.where(rows == i, new, inv)
    out_ref[...] = inv

def chol_inv(g):
    n = g.shape[0]
    return pl.pallas_call(
        chol_inv_kernel,
        out_shape=jax.ShapeDtypeStruct(g.shape, jnp.float32),
        cost_estimate=pl.CostEstimate(flops=4 * n * n * n, bytes_accessed=8 * n * n, transcendentals=n),
    )(g)


def orthonormal(filtered, rows_total):
    partial_gram = jnp.einsum(
        "zvd,zwd->vw", filtered, filtered, precision=lax.Precision.HIGHEST
    )
    gram_matrix = all_sum(partial_gram, ("gx", "gy"))
    inverse = chol_inv(gram_matrix)
    result = jnp.einsum("vw,zwd->zvd", inverse, filtered, precision=lax.Precision.HIGHEST)
    return result * math.sqrt(rows_total)


def local(basis, coupling, cpl_dst, cpl_src):
    column_depth = basis.shape[2]
    vector_count = basis.shape[3]
    block_rows = basis.shape[4]
    rows_total = lax.axis_size("gx") * lax.axis_size("gy") * column_depth * block_rows
    columns = [(1, 1), (0, 1), (2, 1)] + [(dx, 0) for dx in range(3)] + [(dx, 2) for dx in range(3)]
    order = [(3 * dx + dy) * column_depth + z for dx, dy in columns for z in range(column_depth)]
    dense = dense_coupling(coupling[0, 0], cpl_dst[0, 0], cpl_src[0, 0], column_depth, order)
    dense_own = dense[:, :column_depth]
    dense_side = dense[:, column_depth:3 * column_depth]
    dense_low = dense[:, 3 * column_depth:6 * column_depth]
    dense_high = dense[:, 6 * column_depth:]

    def shift(value, axis, step):
        count = lax.axis_size(axis)
        return lax.ppermute(value, axis, [(i, (i + step) % count) for i in range(count)])

    def part(cells, blocks):
        return jnp.einsum("kvj,tkij->tvi", cells, blocks, preferred_element_type=jnp.float32)

    def apply_operator(current):
        rounded = current.astype(jnp.bfloat16)
        left = shift(rounded, "gx", 1)
        right = shift(rounded, "gx", -1)
        image = part(rounded, dense_own)
        strip = jnp.stack([left, rounded, right])
        low = shift(strip, "gy", 1)
        high = shift(strip, "gy", -1)
        image = image + part(jnp.concatenate([left, right]), dense_side)
        image = image + part(low.reshape(3 * column_depth, vector_count, block_rows), dense_low)
        return image + part(high.reshape(3 * column_depth, vector_count, block_rows), dense_high)

    sigma_one = HALF / (LOWEST - CENTER)
    current_basis = basis[0, 0]
    for outer in range(STEPS):
        previous = current_basis
        current = sigma_one / HALF * (apply_operator(previous) - CENTER * previous)
        sigma_now = sigma_one
        for inner in range(1, DEGREE):
            sigma_next = 1.0 / (2.0 / sigma_one - sigma_now)
            image = apply_operator(current)
            following = (
                2.0 * sigma_next / HALF * (image - CENTER * current)
                - sigma_now * sigma_next * previous
            )
            previous, current, sigma_now = (current, following, sigma_next)
        current_basis = orthonormal(current, rows_total)
    return current_basis[None, None]


def solution(mesh):
    placed = (
        P("gx", "gy", None, None, None),
        P("gx", "gy", None, None, None),
        P("gx", "gy", None),
        P("gx", "gy", None),
    )
    return jax.shard_map(
        local,
        mesh=mesh,
        in_specs=placed,
        out_specs=P("gx", "gy", None, None, None),
        check_vma=False,
    )
```

```python
import math

import jax
import jax.numpy as jnp
from jax import lax
from jax.sharding import PartitionSpec as P

DEGREE = 8
STEPS = 2


CENTER = 5.0
HALF = 3.0
LOWEST = 0.5


def with_halo(cells, sides, width):
    for axis, dim in sides:
        count = lax.axis_size(axis)
        head = lax.slice_in_dim(cells, 0, width, axis=dim)
        tail = lax.slice_in_dim(cells, cells.shape[dim] - width, cells.shape[dim], axis=dim)
        cells = jnp.concatenate(
            [
                lax.ppermute(tail, axis, [(i, (i + 1) % count) for i in range(count)]),
                cells,
                lax.ppermute(head, axis, [((i + 1) % count, i) for i in range(count)]),
            ],
            axis=dim,
        )
    return cells


def dense_coupling(matrices, targets, sources, depth, order):
    slots = matrices.shape[0]
    cells = len(order)
    match = (targets[:, None, None] == jnp.arange(depth, dtype=jnp.int32)[None, :, None]) & (
        sources[:, None, None] == jnp.array(order, dtype=jnp.int32)[None, None, :]
    )
    slot_ids = jnp.arange(slots, dtype=jnp.int32)[:, None, None]
    index = jnp.sum(jnp.where(match, slot_ids, 0), axis=0)
    present = jnp.any(match, axis=0)
    flat_index = index.reshape(-1)
    flat_present = present.reshape(-1)
    zero = jnp.zeros(matrices.shape[1:], matrices.dtype)
    blocks = jnp.stack(
        [
            jnp.where(flat_present[c], lax.dynamic_index_in_dim(matrices, flat_index[c], keepdims=False), zero)
            for c in range(depth * cells)
        ]
    ).reshape(depth, cells, matrices.shape[1], matrices.shape[2])
    return lax.optimization_barrier(blocks)


def all_sum(value, axes):
    for axis in axes:
        count = lax.axis_size(axis)
        if count & (count - 1):
            value = lax.psum(value, axis)
            continue

        def swap(v, stride):
            return lax.ppermute(v, axis, [(i, i ^ stride) for i in range(count)])

        stride = 1
        while stride < count:
            if 4 * stride <= count:
                near, far, both = swap(value, stride), swap(value, 2 * stride), swap(value, 3 * stride)
                value = (value + near) + (far + both)
                stride *= 4
            else:
                value = value + swap(value, stride)
                stride *= 2
    return value


def orthonormal(filtered, rows_total):
    partial_gram = jnp.einsum(
        "zvd,zwd->vw", filtered, filtered, precision=lax.Precision.HIGHEST
    )
    gram_matrix = all_sum(partial_gram, ("gx", "gy"))
    factor = jnp.linalg.cholesky(gram_matrix)
    identity = jnp.eye(filtered.shape[1], dtype=jnp.float32)
    inverse = jax.scipy.linalg.solve_triangular(factor, identity, lower=True)
    result = jnp.einsum("vw,zwd->zvd", inverse, filtered, precision=lax.Precision.HIGHEST)
    return result * math.sqrt(rows_total)


def local(basis, coupling, cpl_dst, cpl_src):
    column_depth = basis.shape[2]
    vector_count = basis.shape[3]
    block_rows = basis.shape[4]
    rows_total = lax.axis_size("gx") * lax.axis_size("gy") * column_depth * block_rows
    columns = [(1, 1), (0, 1), (2, 1)] + [(dx, 0) for dx in range(3)] + [(dx, 2) for dx in range(3)]
    order = [(3 * dx + dy) * column_depth + z for dx, dy in columns for z in range(column_depth)]
    dense = dense_coupling(coupling[0, 0], cpl_dst[0, 0], cpl_src[0, 0], column_depth, order)
    dense_own = dense[:, :column_depth]
    dense_side = dense[:, column_depth:3 * column_depth]
    dense_low = dense[:, 3 * column_depth:6 * column_depth]
    dense_high = dense[:, 6 * column_depth:]

    def shift(value, axis, step):
        count = lax.axis_size(axis)
        return lax.ppermute(value, axis, [(i, (i + step) % count) for i in range(count)])

    def part(cells, blocks):
        return jnp.einsum("kvj,tkij->tvi", cells, blocks, preferred_element_type=jnp.float32)

    def apply_operator(current):
        rounded = current.astype(jnp.bfloat16)
        left = shift(rounded, "gx", 1)
        right = shift(rounded, "gx", -1)
        image = part(rounded, dense_own)
        strip = jnp.stack([left, rounded, right])
        low = shift(strip, "gy", 1)
        high = shift(strip, "gy", -1)
        image = image + part(jnp.concatenate([left, right]), dense_side)
        image = image + part(low.reshape(3 * column_depth, vector_count, block_rows), dense_low)
        return image + part(high.reshape(3 * column_depth, vector_count, block_rows), dense_high)

    sigma_one = HALF / (LOWEST - CENTER)
    current_basis = basis[0, 0]
    for outer in range(STEPS):
        previous = current_basis
        current = sigma_one / HALF * (apply_operator(previous) - CENTER * previous)
        sigma_now = sigma_one
        for inner in range(1, DEGREE):
            sigma_next = 1.0 / (2.0 / sigma_one - sigma_now)
            image = apply_operator(current)
            following = (
                2.0 * sigma_next / HALF * (image - CENTER * current)
                - sigma_now * sigma_next * previous
            )
            previous, current, sigma_now = (current, following, sigma_next)
        current_basis = orthonormal(current, rows_total)
    return current_basis[None, None]


def solution(mesh):
    placed = (
        P("gx", "gy", None, None, None),
        P("gx", "gy", None, None, None),
        P("gx", "gy", None),
        P("gx", "gy", None),
    )
    return jax.shard_map(
        local,
        mesh=mesh,
        in_specs=placed,
        out_specs=P("gx", "gy", None, None, None),
        check_vma=False,
    )
```

```python
import math

import jax
import jax.numpy as jnp
from jax import lax
from jax.sharding import PartitionSpec as P

DEGREE = 8
STEPS = 2


CENTER = 5.0
HALF = 3.0
LOWEST = 0.5


def with_halo(cells, sides, width):
    for axis, dim in sides:
        count = lax.axis_size(axis)
        head = lax.slice_in_dim(cells, 0, width, axis=dim)
        tail = lax.slice_in_dim(cells, cells.shape[dim] - width, cells.shape[dim], axis=dim)
        cells = jnp.concatenate(
            [
                lax.ppermute(tail, axis, [(i, (i + 1) % count) for i in range(count)]),
                cells,
                lax.ppermute(head, axis, [((i + 1) % count, i) for i in range(count)]),
            ],
            axis=dim,
        )
    return cells


def dense_coupling(matrices, targets, sources, depth, order):
    slots = matrices.shape[0]
    cells = len(order)
    match = (targets[:, None, None] == jnp.arange(depth, dtype=jnp.int32)[None, :, None]) & (
        sources[:, None, None] == jnp.array(order, dtype=jnp.int32)[None, None, :]
    )
    slot_ids = jnp.arange(slots, dtype=jnp.int32)[:, None, None]
    index = jnp.sum(jnp.where(match, slot_ids, 0), axis=0)
    present = jnp.any(match, axis=0)
    blocks = jnp.take(matrices, index.reshape(-1), axis=0).reshape(
        depth, cells, matrices.shape[1], matrices.shape[2]
    )
    return lax.optimization_barrier(
        jnp.where(present[:, :, None, None], blocks, jnp.zeros((), matrices.dtype))
    )


def all_sum(value, axes):
    for axis in axes:
        count = lax.axis_size(axis)
        if count & (count - 1):
            value = lax.psum(value, axis)
            continue

        def swap(v, stride):
            return lax.ppermute(v, axis, [(i, i ^ stride) for i in range(count)])

        stride = 1
        while stride < count:
            if 4 * stride <= count:
                near, far, both = swap(value, stride), swap(value, 2 * stride), swap(value, 3 * stride)
                value = (value + near) + (far + both)
                stride *= 4
            else:
                value = value + swap(value, stride)
                stride *= 2
    return value


def orthonormal(filtered, rows_total):
    partial_gram = jnp.einsum(
        "zvd,zwd->vw", filtered, filtered, precision=lax.Precision.HIGHEST
    )
    gram_matrix = all_sum(partial_gram, ("gx", "gy"))
    factor = jnp.linalg.cholesky(gram_matrix)
    identity = jnp.eye(filtered.shape[1], dtype=jnp.float32)
    inverse = jax.scipy.linalg.solve_triangular(factor, identity, lower=True)
    result = jnp.einsum("vw,zwd->zvd", inverse, filtered, precision=lax.Precision.HIGHEST)
    return result * math.sqrt(rows_total)


def local(basis, coupling, cpl_dst, cpl_src):
    column_depth = basis.shape[2]
    vector_count = basis.shape[3]
    block_rows = basis.shape[4]
    rows_total = lax.axis_size("gx") * lax.axis_size("gy") * column_depth * block_rows
    columns = [(1, 1), (0, 1), (2, 1)] + [(dx, 0) for dx in range(3)] + [(dx, 2) for dx in range(3)]
    order = [(3 * dx + dy) * column_depth + z for dx, dy in columns for z in range(column_depth)]
    dense = {}

    def shift(value, axis, step):
        count = lax.axis_size(axis)
        return lax.ppermute(value, axis, [(i, (i + step) % count) for i in range(count)])

    def part(cells, blocks):
        return jnp.einsum("kvj,tkij->tvi", cells, blocks, preferred_element_type=jnp.float32)

    def apply_operator(current):
        rounded = current.astype(jnp.bfloat16)
        left = shift(rounded, "gx", 1)
        right = shift(rounded, "gx", -1)
        strip = jnp.stack([left, rounded, right])
        low = shift(strip, "gy", 1)
        high = shift(strip, "gy", -1)
        if not dense:
            matrices = lax.optimization_barrier((coupling[0, 0], left, right))[0]
            full = dense_coupling(matrices, cpl_dst[0, 0], cpl_src[0, 0], column_depth, order)
            dense["own"] = full[:, :column_depth]
            dense["side"] = full[:, column_depth:3 * column_depth]
            dense["low"] = full[:, 3 * column_depth:6 * column_depth]
            dense["high"] = full[:, 6 * column_depth:]
        image = part(rounded, dense["own"])
        image = image + part(jnp.concatenate([left, right]), dense["side"])
        image = image + part(low.reshape(3 * column_depth, vector_count, block_rows), dense["low"])
        return image + part(high.reshape(3 * column_depth, vector_count, block_rows), dense["high"])

    sigma_one = HALF / (LOWEST - CENTER)
    current_basis = basis[0, 0]
    for outer in range(STEPS):
        previous = current_basis
        current = sigma_one / HALF * (apply_operator(previous) - CENTER * previous)
        sigma_now = sigma_one
        for inner in range(1, DEGREE):
            sigma_next = 1.0 / (2.0 / sigma_one - sigma_now)
            image = apply_operator(current)
            following = (
                2.0 * sigma_next / HALF * (image - CENTER * current)
                - sigma_now * sigma_next * previous
            )
            previous, current, sigma_now = (current, following, sigma_next)
        current_basis = orthonormal(current, rows_total)
    return current_basis[None, None]


def solution(mesh):
    placed = (
        P("gx", "gy", None, None, None),
        P("gx", "gy", None, None, None),
        P("gx", "gy", None),
        P("gx", "gy", None),
    )
    return jax.shard_map(
        local,
        mesh=mesh,
        in_specs=placed,
        out_specs=P("gx", "gy", None, None, None),
        check_vma=False,
    )
```

```python
import math

import jax
import jax.numpy as jnp
from jax import lax
from jax.sharding import PartitionSpec as P

DEGREE = 8
STEPS = 2


CENTER = 5.0
HALF = 3.0
LOWEST = 0.5


def with_halo(cells, sides, width):
    for axis, dim in sides:
        count = lax.axis_size(axis)
        head = lax.slice_in_dim(cells, 0, width, axis=dim)
        tail = lax.slice_in_dim(cells, cells.shape[dim] - width, cells.shape[dim], axis=dim)
        cells = jnp.concatenate(
            [
                lax.ppermute(tail, axis, [(i, (i + 1) % count) for i in range(count)]),
                cells,
                lax.ppermute(head, axis, [((i + 1) % count, i) for i in range(count)]),
            ],
            axis=dim,
        )
    return cells


def dense_coupling(matrices, targets, sources, depth, order):
    slots = matrices.shape[0]
    cells = len(order)
    match = (targets[:, None, None] == jnp.arange(depth, dtype=jnp.int32)[None, :, None]) & (
        sources[:, None, None] == jnp.array(order, dtype=jnp.int32)[None, None, :]
    )
    slot_ids = jnp.arange(slots, dtype=jnp.int32)[:, None, None]
    index = jnp.sum(jnp.where(match, slot_ids, 0), axis=0)
    present = jnp.any(match, axis=0)
    blocks = jnp.take(matrices, index.reshape(-1), axis=0).reshape(
        depth, cells, matrices.shape[1], matrices.shape[2]
    )
    return lax.optimization_barrier(
        jnp.where(present[:, :, None, None], blocks, jnp.zeros((), matrices.dtype))
    )


def all_sum(value, axes):
    for axis in axes:
        count = lax.axis_size(axis)
        if count & (count - 1):
            value = lax.psum(value, axis)
            continue

        def swap(v, stride):
            return lax.ppermute(v, axis, [(i, i ^ stride) for i in range(count)])

        stride = 1
        while stride < count:
            if 4 * stride <= count:
                near, far, both = swap(value, stride), swap(value, 2 * stride), swap(value, 3 * stride)
                value = (value + near) + (far + both)
                stride *= 4
            else:
                value = value + swap(value, stride)
                stride *= 2
    return value


def orthonormal(filtered, rows_total):
    partial_gram = jnp.einsum(
        "zvd,zwd->vw", filtered, filtered, precision=lax.Precision.HIGHEST
    )
    gram_matrix = all_sum(partial_gram, ("gx", "gy"))
    factor = jnp.linalg.cholesky(gram_matrix)
    identity = jnp.eye(filtered.shape[1], dtype=jnp.float32)
    inverse = jax.scipy.linalg.solve_triangular(factor, identity, lower=True)
    result = jnp.einsum("vw,zwd->zvd", inverse, filtered, precision=lax.Precision.HIGHEST)
    return result * math.sqrt(rows_total)


def local(basis, coupling, cpl_dst, cpl_src):
    column_depth = basis.shape[2]
    vector_count = basis.shape[3]
    block_rows = basis.shape[4]
    rows_total = lax.axis_size("gx") * lax.axis_size("gy") * column_depth * block_rows
    columns = [(1, 1), (1, 0), (1, 2)] + [(0, dy) for dy in range(3)] + [(2, dy) for dy in range(3)]
    order = [(3 * dx + dy) * column_depth + z for dx, dy in columns for z in range(column_depth)]
    dense = {}

    def shift(value, axis, step):
        count = lax.axis_size(axis)
        return lax.ppermute(value, axis, [(i, (i + step) % count) for i in range(count)])

    def part(cells, blocks):
        return jnp.einsum("kvj,tkij->tvi", cells, blocks, preferred_element_type=jnp.float32)

    def apply_operator(current):
        rounded = current.astype(jnp.bfloat16)
        left = shift(rounded, "gy", 1)
        right = shift(rounded, "gy", -1)
        strip = jnp.stack([left, rounded, right])
        low = shift(strip, "gx", 1)
        high = shift(strip, "gx", -1)
        if not dense:
            matrices = lax.optimization_barrier((coupling[0, 0], left, right))[0]
            full = dense_coupling(matrices, cpl_dst[0, 0], cpl_src[0, 0], column_depth, order)
            dense["own"] = full[:, :column_depth]
            dense["side"] = full[:, column_depth:3 * column_depth]
            dense["low"] = full[:, 3 * column_depth:6 * column_depth]
            dense["high"] = full[:, 6 * column_depth:]
        image = part(rounded, dense["own"])
        image = image + part(jnp.concatenate([left, right]), dense["side"])
        image = image + part(low.reshape(3 * column_depth, vector_count, block_rows), dense["low"])
        return image + part(high.reshape(3 * column_depth, vector_count, block_rows), dense["high"])

    sigma_one = HALF / (LOWEST - CENTER)
    current_basis = basis[0, 0]
    for outer in range(STEPS):
        previous = current_basis
        current = sigma_one / HALF * (apply_operator(previous) - CENTER * previous)
        sigma_now = sigma_one
        for inner in range(1, DEGREE):
            sigma_next = 1.0 / (2.0 / sigma_one - sigma_now)
            image = apply_operator(current)
            following = (
                2.0 * sigma_next / HALF * (image - CENTER * current)
                - sigma_now * sigma_next * previous
            )
            previous, current, sigma_now = (current, following, sigma_next)
        current_basis = orthonormal(current, rows_total)
    return current_basis[None, None]


def solution(mesh):
    placed = (
        P("gx", "gy", None, None, None),
        P("gx", "gy", None, None, None),
        P("gx", "gy", None),
        P("gx", "gy", None),
    )
    return jax.shard_map(
        local,
        mesh=mesh,
        in_specs=placed,
        out_specs=P("gx", "gy", None, None, None),
        check_vma=False,
    )
```

```python
import math

import jax
import jax.numpy as jnp
from jax import lax
from jax.sharding import PartitionSpec as P

DEGREE = 8
STEPS = 2


CENTER = 5.0
HALF = 3.0
LOWEST = 0.5


def with_halo(cells, sides, width):
    for axis, dim in sides:
        count = lax.axis_size(axis)
        head = lax.slice_in_dim(cells, 0, width, axis=dim)
        tail = lax.slice_in_dim(cells, cells.shape[dim] - width, cells.shape[dim], axis=dim)
        cells = jnp.concatenate(
            [
                lax.ppermute(tail, axis, [(i, (i + 1) % count) for i in range(count)]),
                cells,
                lax.ppermute(head, axis, [((i + 1) % count, i) for i in range(count)]),
            ],
            axis=dim,
        )
    return cells


def dense_coupling(matrices, targets, sources, depth, order):
    slots = matrices.shape[0]
    cells = len(order)
    match = (targets[:, None, None] == jnp.arange(depth, dtype=jnp.int32)[None, :, None]) & (
        sources[:, None, None] == jnp.array(order, dtype=jnp.int32)[None, None, :]
    )
    slot_ids = jnp.arange(slots, dtype=jnp.int32)[:, None, None]
    index = jnp.sum(jnp.where(match, slot_ids, 0), axis=0)
    present = jnp.any(match, axis=0)
    blocks = jnp.take(matrices, index.reshape(-1), axis=0).reshape(
        depth, cells, matrices.shape[1], matrices.shape[2]
    )
    return lax.optimization_barrier(
        jnp.where(present[:, :, None, None], blocks, jnp.zeros((), matrices.dtype))
    )


def all_sum(value, axes):
    for axis in axes:
        count = lax.axis_size(axis)
        if count & (count - 1):
            value = lax.psum(value, axis)
            continue

        def swap(v, stride):
            return lax.ppermute(v, axis, [(i, i ^ stride) for i in range(count)])

        stride = 1
        while stride < count:
            if 4 * stride <= count:
                near, far, both = swap(value, stride), swap(value, 2 * stride), swap(value, 3 * stride)
                value = (value + near) + (far + both)
                stride *= 4
            else:
                value = value + swap(value, stride)
                stride *= 2
    return value


def orthonormal(filtered, rows_total):
    partial_gram = jnp.einsum(
        "zvd,zwd->vw", filtered, filtered, precision=lax.Precision.HIGHEST
    )
    gram_matrix = all_sum(partial_gram, ("gx", "gy"))
    factor = jnp.linalg.cholesky(gram_matrix)
    identity = jnp.eye(filtered.shape[1], dtype=jnp.float32)
    inverse = jax.scipy.linalg.solve_triangular(factor, identity, lower=True)
    result = jnp.einsum("vw,zwd->zvd", inverse, filtered, precision=lax.Precision.HIGHEST)
    return result * math.sqrt(rows_total)


def local(basis, coupling, cpl_dst, cpl_src):
    column_depth = basis.shape[2]
    vector_count = basis.shape[3]
    block_rows = basis.shape[4]
    rows_total = lax.axis_size("gx") * lax.axis_size("gy") * column_depth * block_rows
    columns = [(1, 1), (0, 1), (2, 1)] + [(dx, 0) for dx in range(3)] + [(dx, 2) for dx in range(3)]
    order = [(3 * dx + dy) * column_depth + z for dx, dy in columns for z in range(column_depth)]
    dense = {}

    def shift(value, axis, step):
        count = lax.axis_size(axis)
        return lax.ppermute(value, axis, [(i, (i + step) % count) for i in range(count)])

    def part(cells, blocks):
        return jnp.einsum("kvj,tkij->tvi", cells, blocks, preferred_element_type=jnp.float32)

    def apply_operator(current):
        rounded = current.astype(jnp.bfloat16)
        dense_rows = (column_depth, vector_count * block_rows // 128, 128)
        flat = rounded.reshape(dense_rows)
        left_flat = shift(flat, "gx", 1)
        right_flat = shift(flat, "gx", -1)
        strip = jnp.stack([left_flat, flat, right_flat])
        low = shift(strip, "gy", 1).reshape(3, column_depth, vector_count, block_rows)
        high = shift(strip, "gy", -1).reshape(3, column_depth, vector_count, block_rows)
        left = left_flat.reshape(rounded.shape)
        right = right_flat.reshape(rounded.shape)
        if not dense:
            matrices = lax.optimization_barrier((coupling[0, 0], left, right))[0]
            full = dense_coupling(matrices, cpl_dst[0, 0], cpl_src[0, 0], column_depth, order)
            dense["own"] = full[:, :column_depth]
            dense["side"] = full[:, column_depth:3 * column_depth]
            dense["low"] = full[:, 3 * column_depth:6 * column_depth]
            dense["high"] = full[:, 6 * column_depth:]
        image = part(rounded, dense["own"])
        image = image + part(jnp.concatenate([left, right]), dense["side"])
        image = image + part(low.reshape(3 * column_depth, vector_count, block_rows), dense["low"])
        return image + part(high.reshape(3 * column_depth, vector_count, block_rows), dense["high"])

    sigma_one = HALF / (LOWEST - CENTER)
    current_basis = basis[0, 0]
    for outer in range(STEPS):
        previous = current_basis
        current = sigma_one / HALF * (apply_operator(previous) - CENTER * previous)
        sigma_now = sigma_one
        for inner in range(1, DEGREE):
            sigma_next = 1.0 / (2.0 / sigma_one - sigma_now)
            image = apply_operator(current)
            following = (
                2.0 * sigma_next / HALF * (image - CENTER * current)
                - sigma_now * sigma_next * previous
            )
            previous, current, sigma_now = (current, following, sigma_next)
        current_basis = orthonormal(current, rows_total)
    return current_basis[None, None]


def solution(mesh):
    placed = (
        P("gx", "gy", None, None, None),
        P("gx", "gy", None, None, None),
        P("gx", "gy", None),
        P("gx", "gy", None),
    )
    return jax.shard_map(
        local,
        mesh=mesh,
        in_specs=placed,
        out_specs=P("gx", "gy", None, None, None),
        check_vma=False,
    )
```

```python
import math

import jax
import jax.numpy as jnp
from jax import lax
from jax.sharding import PartitionSpec as P

DEGREE = 8
STEPS = 2


CENTER = 5.0
HALF = 3.0
LOWEST = 0.5


def with_halo(cells, sides, width):
    for axis, dim in sides:
        count = lax.axis_size(axis)
        head = lax.slice_in_dim(cells, 0, width, axis=dim)
        tail = lax.slice_in_dim(cells, cells.shape[dim] - width, cells.shape[dim], axis=dim)
        cells = jnp.concatenate(
            [
                lax.ppermute(tail, axis, [(i, (i + 1) % count) for i in range(count)]),
                cells,
                lax.ppermute(head, axis, [((i + 1) % count, i) for i in range(count)]),
            ],
            axis=dim,
        )
    return cells


def dense_coupling(matrices, targets, sources, depth, order):
    slots = matrices.shape[0]
    cells = len(order)
    match = (targets[:, None, None] == jnp.arange(depth, dtype=jnp.int32)[None, :, None]) & (
        sources[:, None, None] == jnp.array(order, dtype=jnp.int32)[None, None, :]
    )
    slot_ids = jnp.arange(slots, dtype=jnp.int32)[:, None, None]
    index = jnp.sum(jnp.where(match, slot_ids, 0), axis=0)
    present = jnp.any(match, axis=0)
    blocks = jnp.take(matrices, index.reshape(-1), axis=0).reshape(
        depth, cells, matrices.shape[1], matrices.shape[2]
    )
    return lax.optimization_barrier(
        jnp.where(present[:, :, None, None], blocks, jnp.zeros((), matrices.dtype))
    )


def all_sum(value, axes):
    for axis in axes:
        count = lax.axis_size(axis)
        if count & (count - 1):
            value = lax.psum(value, axis)
            continue

        def swap(v, stride):
            return lax.ppermute(v, axis, [(i, i ^ stride) for i in range(count)])

        stride = 1
        if (count.bit_length() - 1) % 2:
            value = value + swap(value, stride)
            stride *= 2
        while stride < count:
            if 4 * stride <= count:
                near, far, both = swap(value, stride), swap(value, 2 * stride), swap(value, 3 * stride)
                value = (value + near) + (far + both)
                stride *= 4
            else:
                value = value + swap(value, stride)
                stride *= 2
    return value


def orthonormal(filtered, rows_total):
    partial_gram = jnp.einsum(
        "zvd,zwd->vw", filtered, filtered, precision=lax.Precision.HIGHEST
    )
    gram_matrix = all_sum(partial_gram, ("gx", "gy"))
    factor = jnp.linalg.cholesky(gram_matrix)
    identity = jnp.eye(filtered.shape[1], dtype=jnp.float32)
    inverse = jax.scipy.linalg.solve_triangular(factor, identity, lower=True)
    result = jnp.einsum("vw,zwd->zvd", inverse, filtered, precision=lax.Precision.HIGHEST)
    return result * math.sqrt(rows_total)


def local(basis, coupling, cpl_dst, cpl_src):
    column_depth = basis.shape[2]
    vector_count = basis.shape[3]
    block_rows = basis.shape[4]
    rows_total = lax.axis_size("gx") * lax.axis_size("gy") * column_depth * block_rows
    columns = [(1, 1), (0, 1), (2, 1)] + [(dx, 0) for dx in range(3)] + [(dx, 2) for dx in range(3)]
    order = [(3 * dx + dy) * column_depth + z for dx, dy in columns for z in range(column_depth)]
    dense = {}

    def shift(value, axis, step):
        count = lax.axis_size(axis)
        return lax.ppermute(value, axis, [(i, (i + step) % count) for i in range(count)])

    def part(cells, blocks):
        return jnp.einsum("kvj,tkij->tvi", cells, blocks, preferred_element_type=jnp.float32)

    def apply_operator(current):
        rounded = current.astype(jnp.bfloat16)
        left = shift(rounded, "gx", 1)
        right = shift(rounded, "gx", -1)
        strip = jnp.stack([left, rounded, right])
        low = shift(strip, "gy", 1)
        high = shift(strip, "gy", -1)
        if not dense:
            matrices = lax.optimization_barrier((coupling[0, 0], left, right))[0]
            full = dense_coupling(matrices, cpl_dst[0, 0], cpl_src[0, 0], column_depth, order)
            dense["own"] = full[:, :column_depth]
            dense["side"] = full[:, column_depth:3 * column_depth]
            dense["low"] = full[:, 3 * column_depth:6 * column_depth]
            dense["high"] = full[:, 6 * column_depth:]
        image = part(rounded, dense["own"])
        image = image + part(jnp.concatenate([left, right]), dense["side"])
        image = image + part(low.reshape(3 * column_depth, vector_count, block_rows), dense["low"])
        return image + part(high.reshape(3 * column_depth, vector_count, block_rows), dense["high"])

    sigma_one = HALF / (LOWEST - CENTER)
    current_basis = basis[0, 0]
    for outer in range(STEPS):
        previous = current_basis
        current = sigma_one / HALF * (apply_operator(previous) - CENTER * previous)
        sigma_now = sigma_one
        for inner in range(1, DEGREE):
            sigma_next = 1.0 / (2.0 / sigma_one - sigma_now)
            image = apply_operator(current)
            following = (
                2.0 * sigma_next / HALF * (image - CENTER * current)
                - sigma_now * sigma_next * previous
            )
            previous, current, sigma_now = (current, following, sigma_next)
        current_basis = orthonormal(current, rows_total)
    return current_basis[None, None]


def solution(mesh):
    placed = (
        P("gx", "gy", None, None, None),
        P("gx", "gy", None, None, None),
        P("gx", "gy", None),
        P("gx", "gy", None),
    )
    return jax.shard_map(
        local,
        mesh=mesh,
        in_specs=placed,
        out_specs=P("gx", "gy", None, None, None),
        check_vma=False,
    )
```

```python
import math

import jax
import jax.numpy as jnp
from jax import lax
from jax.sharding import PartitionSpec as P

DEGREE = 8
STEPS = 2


CENTER = 5.0
HALF = 3.0
LOWEST = 0.5


def with_halo(cells, sides, width):
    for axis, dim in sides:
        count = lax.axis_size(axis)
        head = lax.slice_in_dim(cells, 0, width, axis=dim)
        tail = lax.slice_in_dim(cells, cells.shape[dim] - width, cells.shape[dim], axis=dim)
        cells = jnp.concatenate(
            [
                lax.ppermute(tail, axis, [(i, (i + 1) % count) for i in range(count)]),
                cells,
                lax.ppermute(head, axis, [((i + 1) % count, i) for i in range(count)]),
            ],
            axis=dim,
        )
    return cells


def dense_coupling(matrices, targets, sources, depth, order):
    slots = matrices.shape[0]
    cells = len(order)
    match = (targets[:, None, None] == jnp.arange(depth, dtype=jnp.int32)[None, :, None]) & (
        sources[:, None, None] == jnp.array(order, dtype=jnp.int32)[None, None, :]
    )
    slot_ids = jnp.arange(slots, dtype=jnp.int32)[:, None, None]
    index = jnp.sum(jnp.where(match, slot_ids, 0), axis=0)
    present = jnp.any(match, axis=0)
    blocks = jnp.take(matrices, index.reshape(-1), axis=0).reshape(
        depth, cells, matrices.shape[1], matrices.shape[2]
    )
    return lax.optimization_barrier(
        jnp.where(present[:, :, None, None], blocks, jnp.zeros((), matrices.dtype))
    )


def all_sum(value, axes):
    for axis in axes:
        count = lax.axis_size(axis)
        if count & (count - 1):
            value = lax.psum(value, axis)
            continue

        def swap(v, stride):
            return lax.ppermute(v, axis, [(i, i ^ stride) for i in range(count)])

        stride = 1
        while stride < count:
            if 4 * stride <= count:
                near, far, both = swap(value, stride), swap(value, 2 * stride), swap(value, 3 * stride)
                value = (value + near) + (far + both)
                stride *= 4
            else:
                value = value + swap(value, stride)
                stride *= 2
    return value


def orthonormal(filtered, rows_total):
    partial_gram = jnp.einsum(
        "zvd,zwd->vw", filtered, filtered, precision=lax.Precision.HIGHEST
    )
    gram_matrix = all_sum(partial_gram, ("gx", "gy"))
    factor = jnp.linalg.cholesky(gram_matrix)
    depth, vectors, rows = filtered.shape
    stacked = jnp.transpose(filtered, (1, 0, 2)).reshape(vectors, depth * rows)
    solved = lax.linalg.triangular_solve(factor, stacked, left_side=True, lower=True)
    result = jnp.transpose(solved.reshape(vectors, depth, rows), (1, 0, 2))
    return result * math.sqrt(rows_total)


def local(basis, coupling, cpl_dst, cpl_src):
    column_depth = basis.shape[2]
    vector_count = basis.shape[3]
    block_rows = basis.shape[4]
    rows_total = lax.axis_size("gx") * lax.axis_size("gy") * column_depth * block_rows
    columns = [(1, 1), (0, 1), (2, 1)] + [(dx, 0) for dx in range(3)] + [(dx, 2) for dx in range(3)]
    order = [(3 * dx + dy) * column_depth + z for dx, dy in columns for z in range(column_depth)]
    dense = {}

    def shift(value, axis, step):
        count = lax.axis_size(axis)
        return lax.ppermute(value, axis, [(i, (i + step) % count) for i in range(count)])

    def part(cells, blocks):
        return jnp.einsum("kvj,tkij->tvi", cells, blocks, preferred_element_type=jnp.float32)

    def apply_operator(current):
        rounded = current.astype(jnp.bfloat16)
        left = shift(rounded, "gx", 1)
        right = shift(rounded, "gx", -1)
        strip = jnp.stack([left, rounded, right])
        low = shift(strip, "gy", 1)
        high = shift(strip, "gy", -1)
        if not dense:
            matrices = lax.optimization_barrier((coupling[0, 0], left, right))[0]
            full = dense_coupling(matrices, cpl_dst[0, 0], cpl_src[0, 0], column_depth, order)
            dense["own"] = full[:, :column_depth]
            dense["side"] = full[:, column_depth:3 * column_depth]
            dense["low"] = full[:, 3 * column_depth:6 * column_depth]
            dense["high"] = full[:, 6 * column_depth:]
        image = part(rounded, dense["own"])
        image = image + part(jnp.concatenate([left, right]), dense["side"])
        image = image + part(low.reshape(3 * column_depth, vector_count, block_rows), dense["low"])
        return image + part(high.reshape(3 * column_depth, vector_count, block_rows), dense["high"])

    sigma_one = HALF / (LOWEST - CENTER)
    current_basis = basis[0, 0]
    for outer in range(STEPS):
        previous = current_basis
        current = sigma_one / HALF * (apply_operator(previous) - CENTER * previous)
        sigma_now = sigma_one
        for inner in range(1, DEGREE):
            sigma_next = 1.0 / (2.0 / sigma_one - sigma_now)
            image = apply_operator(current)
            following = (
                2.0 * sigma_next / HALF * (image - CENTER * current)
                - sigma_now * sigma_next * previous
            )
            previous, current, sigma_now = (current, following, sigma_next)
        current_basis = orthonormal(current, rows_total)
    return current_basis[None, None]


def solution(mesh):
    placed = (
        P("gx", "gy", None, None, None),
        P("gx", "gy", None, None, None),
        P("gx", "gy", None),
        P("gx", "gy", None),
    )
    return jax.shard_map(
        local,
        mesh=mesh,
        in_specs=placed,
        out_specs=P("gx", "gy", None, None, None),
        check_vma=False,
    )
```

```python
import math

import jax
import jax.numpy as jnp
from jax import lax
from jax.sharding import PartitionSpec as P

DEGREE = 8
STEPS = 2


CENTER = 5.0
HALF = 3.0
LOWEST = 0.5


def with_halo(cells, sides, width):
    for axis, dim in sides:
        count = lax.axis_size(axis)
        head = lax.slice_in_dim(cells, 0, width, axis=dim)
        tail = lax.slice_in_dim(cells, cells.shape[dim] - width, cells.shape[dim], axis=dim)
        cells = jnp.concatenate(
            [
                lax.ppermute(tail, axis, [(i, (i + 1) % count) for i in range(count)]),
                cells,
                lax.ppermute(head, axis, [((i + 1) % count, i) for i in range(count)]),
            ],
            axis=dim,
        )
    return cells


def dense_coupling(matrices, targets, sources, depth, order):
    slots = matrices.shape[0]
    cells = len(order)
    match = (targets[:, None, None] == jnp.arange(depth, dtype=jnp.int32)[None, :, None]) & (
        sources[:, None, None] == jnp.array(order, dtype=jnp.int32)[None, None, :]
    )
    slot_ids = jnp.arange(slots, dtype=jnp.int32)[:, None, None]
    index = jnp.sum(jnp.where(match, slot_ids, 0), axis=0)
    present = jnp.any(match, axis=0)
    blocks = jnp.take(matrices, index.reshape(-1), axis=0).reshape(
        depth, cells, matrices.shape[1], matrices.shape[2]
    )
    return lax.optimization_barrier(
        jnp.where(present[:, :, None, None], blocks, jnp.zeros((), matrices.dtype))
    )


def all_sum(value, axes):
    for axis in axes:
        count = lax.axis_size(axis)
        if count & (count - 1):
            value = lax.psum(value, axis)
            continue

        def swap(v, stride):
            return lax.ppermute(v, axis, [(i, i ^ stride) for i in range(count)])

        stride = 1
        if (count.bit_length() - 1) % 2:
            value = value + swap(value, stride)
            stride *= 2
        while stride < count:
            if 4 * stride <= count:
                near, far, both = swap(value, stride), swap(value, 2 * stride), swap(value, 3 * stride)
                value = (value + near) + (far + both)
                stride *= 4
            else:
                value = value + swap(value, stride)
                stride *= 2
    return value


def orthonormal(filtered, rows_total):
    partial_gram = jnp.einsum(
        "zvd,zwd->vw", filtered, filtered, precision=lax.Precision.HIGHEST
    )
    gram_matrix = all_sum(partial_gram, ("gx", "gy"))
    factor = jnp.linalg.cholesky(gram_matrix)
    depth, vectors, rows = filtered.shape
    stacked = jnp.transpose(filtered, (1, 0, 2)).reshape(vectors, depth * rows)
    solved = lax.linalg.triangular_solve(factor, stacked, left_side=True, lower=True)
    result = jnp.transpose(solved.reshape(vectors, depth, rows), (1, 0, 2))
    return result * math.sqrt(rows_total)


def local(basis, coupling, cpl_dst, cpl_src):
    column_depth = basis.shape[2]
    vector_count = basis.shape[3]
    block_rows = basis.shape[4]
    rows_total = lax.axis_size("gx") * lax.axis_size("gy") * column_depth * block_rows
    columns = [(1, 1), (0, 1), (2, 1)] + [(dx, 0) for dx in range(3)] + [(dx, 2) for dx in range(3)]
    order = [(3 * dx + dy) * column_depth + z for dx, dy in columns for z in range(column_depth)]
    dense = {}

    def shift(value, axis, step):
        count = lax.axis_size(axis)
        return lax.ppermute(value, axis, [(i, (i + step) % count) for i in range(count)])

    def part(cells, blocks):
        return jnp.einsum("kvj,tkij->tvi", cells, blocks, preferred_element_type=jnp.float32)

    def apply_operator(current):
        rounded = current.astype(jnp.bfloat16)
        left = shift(rounded, "gx", 1)
        right = shift(rounded, "gx", -1)
        strip = jnp.stack([left, rounded, right])
        low = shift(strip, "gy", 1)
        high = shift(strip, "gy", -1)
        if not dense:
            matrices = lax.optimization_barrier((coupling[0, 0], left, right))[0]
            full = dense_coupling(matrices, cpl_dst[0, 0], cpl_src[0, 0], column_depth, order)
            dense["own"] = full[:, :column_depth]
            dense["side"] = full[:, column_depth:3 * column_depth]
            dense["low"] = full[:, 3 * column_depth:6 * column_depth]
            dense["high"] = full[:, 6 * column_depth:]
        image = part(rounded, dense["own"])
        image = image + part(jnp.concatenate([left, right]), dense["side"])
        image = image + part(low.reshape(3 * column_depth, vector_count, block_rows), dense["low"])
        return image + part(high.reshape(3 * column_depth, vector_count, block_rows), dense["high"])

    sigma_one = HALF / (LOWEST - CENTER)
    current_basis = basis[0, 0]
    for outer in range(STEPS):
        previous = current_basis
        current = sigma_one / HALF * (apply_operator(previous) - CENTER * previous)
        sigma_now = sigma_one
        for inner in range(1, DEGREE):
            sigma_next = 1.0 / (2.0 / sigma_one - sigma_now)
            image = apply_operator(current)
            following = (
                2.0 * sigma_next / HALF * (image - CENTER * current)
                - sigma_now * sigma_next * previous
            )
            previous, current, sigma_now = (current, following, sigma_next)
        current_basis = orthonormal(current, rows_total)
    return current_basis[None, None]


def solution(mesh):
    placed = (
        P("gx", "gy", None, None, None),
        P("gx", "gy", None, None, None),
        P("gx", "gy", None),
        P("gx", "gy", None),
    )
    return jax.shard_map(
        local,
        mesh=mesh,
        in_specs=placed,
        out_specs=P("gx", "gy", None, None, None),
        check_vma=False,
    )
```
